32 devices in a mesh: dp: 2 (over x), tensor: 16 (over z, y, core).
Axes of the slice: x: 2, y: 2, z: 4, core: 2. Of those that a mesh axis runs over, the one named last changes fastest.
Arguments:
- hidden: bfloat16 [384, 2048], P(('dp', 'tensor')), may hold values from -20 to 20
- gain: float32 [2048], replicated, may hold values from 0.1 to 1.9
- head_weight: bfloat16 [2048, 76032], P(None, 'tensor'), may hold values from -8 to 8
- targets: int32 [384], P(('dp', 'tensor')), may hold values from 0 to 76031
- short_lengths: int32 [2], replicated, may hold values from 16 to 64
- owner: int32 [3], replicated, may hold values from 0 to 1, as said below
Outputs:
- logprob: float32 [384], P(('dp', 'tensor'))
- entropy: float32 [384], P(('dp', 'tensor'))
- seq_scores: float32 [2, 2, 3], P('dp')
The draws below stay inside these ranges and needn't reach their ends.
Inputs may be any that keep to these rules, and one draw needn't show every extreme that they name: `owner`: every dp index owns some sequence.
All inputs are finite; a program needn't handle non-finite values.
Results may differ from the reference program's by a relative error of at most 0.0028.
Values may be sent and summed in bfloat16 or wider, within the bound.
No kernel may reach another device: no remote copies, remote signals or barrier semaphores. Data moves between devices by JAX's collectives and lax.ppermute only.
A program may use at most 64 MiB of HBM per device.

```python
import math
import jax
import jax.numpy as jnp
import numpy as np
from jax import lax

D = 2048
VOCAB = 76032
SLOT = 64
TOKENS = 384
SHORTS = 2
LONG = 256
NSEQ = 3
ROWS_DP = 192
N_DP = 2


def draw_hidden(key, part):
    base = jax.random.normal(jax.random.fold_in(key, 1), (TOKENS, D), jnp.float32)
    return base.astype(jnp.bfloat16)


def draw_head_weight(key, part):
    column = jnp.arange(VOCAB).astype(jnp.float32) / VOCAB
    column_scale = jnp.exp(jax.random.uniform(jax.random.fold_in(key, 4), (VOCAB,), jnp.float32, -0.916291, 0.916291))
    ramp = 0.7 + 0.9 * column
    noise = jax.random.normal(jax.random.fold_in(key, 5), (D, VOCAB), jnp.float32)
    weight = noise * (ramp * column_scale)[None, :] / jnp.sqrt(jnp.float32(D))
    return weight.astype(jnp.bfloat16)


def draw_short_lengths(key, part):
    lengths = jax.random.randint(jax.random.fold_in(key, 11), (SHORTS,), SLOT // 4, SLOT + 1)
    place = jax.random.randint(jax.random.fold_in(key, 12), (), 0, SHORTS)
    lengths = lengths.at[place].set(SLOT)
    lengths = lengths.at[(place + 1) % SHORTS].set(SLOT // 4)
    return lengths.astype(jnp.int32)


def draw_owner(key, part):
    order = jax.random.permutation(jax.random.fold_in(key, 13), NSEQ)
    return (order % N_DP).astype(jnp.int32)


def place_ends(array, key, smallest, high):
    longest = array.shape.index(max(array.shape))
    spots = []
    for shift in (0, 1):
        where = [jax.random.randint(jax.random.fold_in(key, axis), (), 0, length) for axis, length in enumerate(array.shape)]
        where[longest] = (where[longest] + shift) % array.shape[longest]
        spots.append(tuple(where))
    return array.at[spots[0]].set(smallest).at[spots[1]].set(high)


def wide_ids(rng, shape, number_of, slope):
    portions = [min(1 << octave, number_of + 1 - (1 << octave)) * (1 << 20) // math.isqrt((1 << octave) ** slope) + 1 for octave in range((number_of + 1).bit_length()) if 1 << octave <= number_of]
    deviation = 1 + sum(portions) // (1 << 30)
    listing = np.cumsum(np.array([max(1, weight // deviation) for weight in portions]))
    lot = jax.random.randint(jax.random.fold_in(rng, 1), shape, 0, int(listing[len(portions) - 1]))
    start = jnp.left_shift(1, jnp.searchsorted(jnp.asarray(listing, jnp.int32), lot, side="right").astype(jnp.int32))
    grade = start - 1 + jax.random.randint(jax.random.fold_in(rng, 4), shape, 0, 1 << 30) % jnp.minimum(start, number_of + 1 - start)
    return jax.random.permutation(jax.random.fold_in(rng, 2), number_of)[grade].astype(jnp.int32)


def setup_inputs(seed: int = 0) -> dict:
    seeds = jax.random.split(jax.random.key(seed), 7)
    hidden = draw_hidden(jax.random.fold_in(seeds[6], 71), 0)
    gain = jnp.clip(1.0 + 0.18 * jax.random.normal(seeds[1], (D,), jnp.float32), 0.1, 1.9)
    head_weight = draw_head_weight(jax.random.fold_in(seeds[6], 71), 0)
    targets = place_ends(wide_ids(seeds[3], (TOKENS,), VOCAB, 2), jax.random.fold_in(seeds[3], 3), 0, VOCAB - 1).astype(jnp.int32)
    short_lengths = draw_short_lengths(jax.random.fold_in(seeds[6], 71), 0)
    owner = draw_owner(jax.random.fold_in(seeds[6], 71), 0)
    return {"hidden": hidden, "gain": gain, "head_weight": head_weight, "targets": targets, "short_lengths": short_lengths, "owner": owner}


def block_stats(normed_rows, weight, target_rows):
    logits = jnp.dot(normed_rows, weight, preferred_element_type=jnp.float32)
    row_top = lax.optimization_barrier(jnp.max(logits, axis=1))
    shifted = logits - row_top[:, None]
    weights_exp = jnp.exp(shifted)
    row_total = lax.optimization_barrier(jnp.sum(weights_exp, axis=1))
    spread = lax.optimization_barrier(jnp.sum(weights_exp * shifted, axis=1))
    picked = jnp.take_along_axis(logits, target_rows[:, None].astype(jnp.int32), axis=1)[:, 0]
    return (picked - row_top - jnp.log(row_total), jnp.log(row_total) - spread / row_total)

def reference(hidden, gain, head_weight, targets, short_lengths, owner):
    values = hidden.astype(jnp.float32)
    normed = (values * lax.rsqrt(lax.optimization_barrier(jnp.mean(values * values, axis=1, keepdims=True)) + 1e-06) * gain).astype(jnp.bfloat16)
    block_count = TOKENS // ROWS_DP
    logprob, entropy = lax.map(lambda packed: block_stats(packed[0], head_weight, packed[1]), (normed.reshape(block_count, ROWS_DP, D), targets.reshape(block_count, ROWS_DP)))
    logprob = logprob.reshape(TOKENS)
    entropy = entropy.reshape(TOKENS)
    row_ids = jnp.arange(TOKENS, dtype=jnp.int32)
    past_long = row_ids - LONG
    sequence = jnp.where(row_ids < LONG, 0, 1 + past_long // SLOT).astype(jnp.int32)
    slot_pos = past_long % SLOT
    seq_lengths = jnp.concatenate([jnp.full((1,), LONG, jnp.int32), short_lengths.astype(jnp.int32)])
    is_live = (row_ids < LONG) | (slot_pos < seq_lengths[sequence])
    logprob = jnp.where(is_live, logprob, jnp.float32(0.0))
    entropy = jnp.where(is_live, entropy, jnp.float32(0.0))
    member = sequence[:, None] == jnp.arange(NSEQ, dtype=jnp.int32)[None, :]
    seq_sums = jnp.stack([lax.optimization_barrier(jnp.sum(jnp.where(member, logprob[:, None], jnp.float32(0.0)), axis=0)), lax.optimization_barrier(jnp.sum(jnp.where(member, entropy[:, None], jnp.float32(0.0)), axis=0))])
    seq_means = seq_sums / seq_lengths.astype(jnp.float32)[None, :]
    is_owner = owner[None, :] == jnp.arange(N_DP, dtype=jnp.int32)[:, None]
    seq_scores = jnp.where(is_owner[:, None, :], seq_means[None, :, :], jnp.float32(0.0))
    return (logprob, entropy, seq_scores)
```

```python
import jax
import jax.numpy as jnp
from jax import lax
from jax.sharding import PartitionSpec as P

SLOT = 64
DIGIT = 256
PAD_COLS = 128


def local_stats(normed_rows, target_rows, weight, offset):
    logits = jnp.dot(normed_rows, weight, preferred_element_type=jnp.float32)
    row_top = jnp.max(logits, axis=1)
    shifted = logits - row_top[:, None]
    weights_exp = jnp.exp(shifted)
    row_total = jnp.sum(weights_exp, axis=1)
    spread = jnp.sum(weights_exp * shifted, axis=1)
    columns = lax.iota(jnp.int32, weight.shape[1]) + offset
    is_target = target_rows[:, None] == columns[None, :]
    picked = jnp.sum(jnp.where(is_target, logits, jnp.float32(0.0)), axis=1)
    return jnp.stack([row_top, row_total, spread, picked])


def body(hidden, gain, head_weight, targets, short_lengths, owner):
    own_rows, features = hidden.shape
    dp_pos = lax.axis_index("dp")
    dp_count = lax.axis_size("dp")
    tensor_pos = lax.axis_index("tensor")
    tensor_count = lax.axis_size("tensor")
    offset = tensor_pos * head_weight.shape[1]
    values = hidden.astype(jnp.float32)
    normed = (
        values * lax.rsqrt(jnp.mean(values * values, axis=1, keepdims=True) + 1e-06) * gain
    ).astype(jnp.bfloat16)

    digits = jnp.stack(
        [targets % DIGIT, (targets // DIGIT) % DIGIT, targets // (DIGIT * DIGIT)], axis=1
    ).astype(jnp.bfloat16)
    packed = jnp.concatenate(
        [normed, digits, jnp.zeros((own_rows, PAD_COLS - 3), jnp.bfloat16)], axis=1
    )
    gathered = lax.all_gather(packed, "tensor", axis=0, tiled=True)
    rows_normed = gathered[:, :features]
    got = gathered[:, features:features + 3].astype(jnp.int32)
    rows_targets = got[:, 0] + DIGIT * got[:, 1] + (DIGIT * DIGIT) * got[:, 2]

    stats = local_stats(rows_normed, rows_targets, head_weight, offset)
    group_rows = stats.shape[1]
    devices = dp_count * tensor_count
    sent = jnp.broadcast_to(stats[None], (devices,) + stats.shape)
    everything = lax.all_to_all(sent, ("dp", "tensor"), 0, 0, tiled=True)
    everything = everything.reshape(dp_count, tensor_count, 4, group_rows)
    tops = everything[:, :, 0]
    joint = jnp.max(tops, axis=1)
    factor = jnp.exp(tops - joint[:, None, :])
    totals = everything[:, :, 1]
    row_total = jnp.sum(totals * factor, axis=1)
    spread = jnp.sum(factor * (everything[:, :, 2] + totals * (tops - joint[:, None, :])), axis=1)
    picked = jnp.sum(everything[:, :, 3], axis=1)
    total_rows = dp_count * group_rows
    row_top = joint.reshape(total_rows)
    row_total = row_total.reshape(total_rows)
    spread = spread.reshape(total_rows)
    picked = picked.reshape(total_rows)

    log_total = jnp.log(row_total)
    logprob = picked - row_top - log_total
    entropy = log_total - spread / row_total
    short_count = short_lengths.shape[0]
    long_len = total_rows - short_count * SLOT
    row_ids = lax.iota(jnp.int32, total_rows)
    past_long = row_ids - long_len
    sequence = jnp.where(row_ids < long_len, 0, 1 + past_long // SLOT)
    slot_pos = past_long % SLOT
    seq_lengths = jnp.concatenate([jnp.full((1,), long_len, jnp.int32), short_lengths])
    member = sequence[:, None] == lax.iota(jnp.int32, short_count + 1)[None, :]
    row_length = jnp.sum(jnp.where(member, seq_lengths[None, :], 0), axis=1)
    is_live = (row_ids < long_len) | (slot_pos < row_length)
    logprob = jnp.where(is_live, logprob, jnp.float32(0.0))
    entropy = jnp.where(is_live, entropy, jnp.float32(0.0))
    seq_sums = jnp.stack(
        [
            jnp.sum(jnp.where(member, logprob[:, None], jnp.float32(0.0)), axis=0),
            jnp.sum(jnp.where(member, entropy[:, None], jnp.float32(0.0)), axis=0),
        ]
    )
    seq_means = seq_sums / seq_lengths.astype(jnp.float32)[None, :]
    is_owner = owner == dp_pos
    seq_scores = jnp.where(is_owner[None, :], seq_means, jnp.float32(0.0))[None, :, :]
    start = (dp_pos * tensor_count + tensor_pos) * own_rows
    own_logprob = lax.dynamic_slice_in_dim(logprob, start, own_rows)
    own_entropy = lax.dynamic_slice_in_dim(entropy, start, own_rows)
    return (own_logprob, own_entropy, seq_scores)


def solution(mesh):
    return jax.shard_map(
        body,
        mesh=mesh,
        in_specs=(P(("dp", "tensor"), None), P(), P(None, "tensor"), P(("dp", "tensor")), P(), P()),
        out_specs=(P(("dp", "tensor")), P(("dp", "tensor")), P("dp", None, None)),
        check_vma=False,
    )
```

```python
import functools

import jax
import jax.numpy as jnp
from jax import lax
from jax.experimental import pallas as pl
from jax.experimental.pallas import tpu as pltpu

from jax.sharding import PartitionSpec as P

SLOT = 64
FLOOR = -1e30
DIGIT = 256
PAD_COLS = 128


def stats_kernel(rows_ref, tgt_ref, w_ref, o_ref, m_ref, s_ref, sp_ref, pk_ref, *, width, block):
    j = pl.program_id(0)

    @pl.when(j == 0)
    def _():
        m_ref[...] = jnp.full(m_ref.shape, FLOOR, jnp.float32)
        s_ref[...] = jnp.zeros(s_ref.shape, jnp.float32)
        sp_ref[...] = jnp.zeros(sp_ref.shape, jnp.float32)
        pk_ref[...] = jnp.zeros(pk_ref.shape, jnp.float32)

    logits = lax.dot_general(
        rows_ref[...], w_ref[...], (((1,), (1,)), ((), ())), preferred_element_type=jnp.float32
    )
    cols = j * block + lax.broadcasted_iota(jnp.int32, logits.shape, 1)
    hit = cols == tgt_ref[...]
    if width % block:
        valid = cols < width
        logits = jnp.where(valid, logits, FLOOR)
        hit = hit & valid
    m_old = m_ref[...]
    m_new = jnp.maximum(m_old, jnp.max(logits, axis=1, keepdims=True))
    shifted = logits - m_new
    e = jnp.exp(shifted)
    factor = jnp.exp(m_old - m_new)
    s_old = s_ref[...]
    s_ref[...] = s_old * factor + jnp.sum(e, axis=1, keepdims=True)
    sp_ref[...] = factor * (sp_ref[...] + s_old * (m_old - m_new)) + jnp.sum(e * shifted, axis=1, keepdims=True)
    m_ref[...] = m_new
    pk_ref[...] += jnp.sum(jnp.where(hit, logits, 0.0), axis=1, keepdims=True)

    @pl.when(j == pl.num_programs(0) - 1)
    def _():
        o_ref[:, 0:1] = m_ref[...]
        o_ref[:, 1:2] = s_ref[...]
        o_ref[:, 2:3] = sp_ref[...]
        o_ref[:, 3:4] = pk_ref[...]


def pick_block(width):
    for block in (528, 512, 432, 384):
        if width % block == 0:
            return block
    return width if width <= 1536 else 512


def fused_stats(rows, feat, local_targets, weight_t):
    nrows = rows.shape[0]
    width = weight_t.shape[0]
    block = pick_block(width)
    steps = pl.cdiv(width, block)
    out = pl.pallas_call(
        functools.partial(stats_kernel, width=width, block=block),
        grid=(steps,),
        in_specs=[
            pl.BlockSpec((nrows, feat), lambda j: (0, 0)),
            pl.BlockSpec((nrows, 1), lambda j: (0, 0)),
            pl.BlockSpec((block, feat), lambda j: (j, 0)),
        ],
        out_specs=pl.BlockSpec((nrows, 128), lambda j: (0, 0)),
        out_shape=jax.ShapeDtypeStruct((nrows, 128), jnp.float32),
        scratch_shapes=[pltpu.VMEM((nrows, 1), jnp.float32)] * 4,
        compiler_params=pltpu.CompilerParams(dimension_semantics=("arbitrary",)),
    )(rows, local_targets, weight_t)
    return out[:, :4].T


def body(hidden, gain, head_weight, targets, short_lengths, owner):
    own_rows, features = hidden.shape
    dp_pos = lax.axis_index("dp")
    dp_count = lax.axis_size("dp")
    tensor_pos = lax.axis_index("tensor")
    tensor_count = lax.axis_size("tensor")
    offset = tensor_pos * head_weight.shape[1]
    values = hidden.astype(jnp.float32)
    normed = (
        values * lax.rsqrt(jnp.mean(values * values, axis=1, keepdims=True) + 1e-06) * gain
    ).astype(jnp.bfloat16)

    digits = jnp.stack(
        [targets % DIGIT, (targets // DIGIT) % DIGIT, targets // (DIGIT * DIGIT)], axis=1
    ).astype(jnp.bfloat16)
    packed = jnp.concatenate(
        [normed, digits, jnp.zeros((own_rows, PAD_COLS - 3), jnp.bfloat16)], axis=1
    )
    gathered = lax.all_gather(packed, "tensor", axis=0, tiled=True)
    got = gathered[:, features:features + 3].astype(jnp.int32)
    rows_targets = got[:, 0] + DIGIT * got[:, 1] + (DIGIT * DIGIT) * got[:, 2]

    stats = fused_stats(gathered, features, (rows_targets - offset)[:, None], head_weight.T)
    group_rows = stats.shape[1]
    devices = dp_count * tensor_count
    sent = jnp.broadcast_to(stats[None], (devices,) + stats.shape)
    everything = lax.all_to_all(sent, ("dp", "tensor"), 0, 0, tiled=True)
    everything = everything.reshape(dp_count, tensor_count, 4, group_rows)
    tops = everything[:, :, 0]
    joint = jnp.max(tops, axis=1)
    factor = jnp.exp(tops - joint[:, None, :])
    totals = everything[:, :, 1]
    row_total = jnp.sum(totals * factor, axis=1)
    spread = jnp.sum(factor * (everything[:, :, 2] + totals * (tops - joint[:, None, :])), axis=1)
    picked = jnp.sum(everything[:, :, 3], axis=1)
    total_rows = dp_count * group_rows
    row_top = joint.reshape(total_rows)
    row_total = row_total.reshape(total_rows)
    spread = spread.reshape(total_rows)
    picked = picked.reshape(total_rows)

    log_total = jnp.log(row_total)
    logprob = picked - row_top - log_total
    entropy = log_total - spread / row_total
    short_count = short_lengths.shape[0]
    long_len = total_rows - short_count * SLOT
    row_ids = lax.iota(jnp.int32, total_rows)
    past_long = row_ids - long_len
    sequence = jnp.where(row_ids < long_len, 0, 1 + past_long // SLOT)
    slot_pos = past_long % SLOT
    seq_lengths = jnp.concatenate([jnp.full((1,), long_len, jnp.int32), short_lengths])
    member = sequence[:, None] == lax.iota(jnp.int32, short_count + 1)[None, :]
    row_length = jnp.sum(jnp.where(member, seq_lengths[None, :], 0), axis=1)
    is_live = (row_ids < long_len) | (slot_pos < row_length)
    logprob = jnp.where(is_live, logprob, jnp.float32(0.0))
    entropy = jnp.where(is_live, entropy, jnp.float32(0.0))
    seq_sums = jnp.stack(
        [
            jnp.sum(jnp.where(member, logprob[:, None], jnp.float32(0.0)), axis=0),
            jnp.sum(jnp.where(member, entropy[:, None], jnp.float32(0.0)), axis=0),
        ]
    )
    seq_means = seq_sums / seq_lengths.astype(jnp.float32)[None, :]
    is_owner = owner == dp_pos
    seq_scores = jnp.where(is_owner[None, :], seq_means, jnp.float32(0.0))[None, :, :]
    start = (dp_pos * tensor_count + tensor_pos) * own_rows
    own_logprob = lax.dynamic_slice_in_dim(logprob, start, own_rows)
    own_entropy = lax.dynamic_slice_in_dim(entropy, start, own_rows)
    return (own_logprob, own_entropy, seq_scores)


def solution(mesh):
    return jax.shard_map(
        body,
        mesh=mesh,
        in_specs=(P(("dp", "tensor"), None), P(), P(None, "tensor"), P(("dp", "tensor")), P(), P()),
        out_specs=(P(("dp", "tensor")), P(("dp", "tensor")), P("dp", None, None)),
        check_vma=False,
    )
```

```python
import functools

import jax
import jax.numpy as jnp
from jax import lax
from jax.experimental import pallas as pl
from jax.experimental.pallas import tpu as pltpu

from jax.sharding import PartitionSpec as P

SLOT = 64
FLOOR = -1e30
DIGIT = 256
PAD_COLS = 128


def stats_kernel(rows_t_ref, tgt_ref, w_ref, o_ref, m_ref, s_ref, sp_ref, pk_ref, *, width, block):
    j = pl.program_id(0)

    @pl.when(j == 0)
    def _():
        m_ref[...] = jnp.full(m_ref.shape, FLOOR, jnp.float32)
        s_ref[...] = jnp.zeros(s_ref.shape, jnp.float32)
        sp_ref[...] = jnp.zeros(sp_ref.shape, jnp.float32)
        pk_ref[...] = jnp.zeros(pk_ref.shape, jnp.float32)

    logits = jnp.dot(w_ref[...], rows_t_ref[...], preferred_element_type=jnp.float32)
    cols = j * block + lax.broadcasted_iota(jnp.int32, logits.shape, 0)
    hit = cols == tgt_ref[...]
    if width % block:
        valid = cols < width
        logits = jnp.where(valid, logits, FLOOR)
        hit = hit & valid
    m_old = m_ref[...]
    m_new = jnp.maximum(m_old, jnp.max(logits, axis=0, keepdims=True))
    shifted = logits - m_new
    e = jnp.exp(shifted)
    factor = jnp.exp(m_old - m_new)
    s_old = s_ref[...]
    s_ref[...] = s_old * factor + jnp.sum(e, axis=0, keepdims=True)
    sp_ref[...] = factor * (sp_ref[...] + s_old * (m_old - m_new)) + jnp.sum(e * shifted, axis=0, keepdims=True)
    m_ref[...] = m_new
    pk_ref[...] += jnp.sum(jnp.where(hit, logits, 0.0), axis=0, keepdims=True)

    @pl.when(j == pl.num_programs(0) - 1)
    def _():
        o_ref[0:1, :] = m_ref[...]
        o_ref[1:2, :] = s_ref[...]
        o_ref[2:3, :] = sp_ref[...]
        o_ref[3:4, :] = pk_ref[...]


def pick_block(width):
    for block in (528, 512, 432, 384):
        if width % block == 0:
            return block
    return width if width <= 1536 else 512


def fused_stats(rows_t, local_targets, weight_t):
    feat, nrows = rows_t.shape
    width = weight_t.shape[0]
    block = pick_block(width)
    steps = pl.cdiv(width, block)
    return pl.pallas_call(
        functools.partial(stats_kernel, width=width, block=block),
        grid=(steps,),
        in_specs=[
            pl.BlockSpec((feat, nrows), lambda j: (0, 0)),
            pl.BlockSpec((1, nrows), lambda j: (0, 0)),
            pl.BlockSpec((block, feat), lambda j: (j, 0)),
        ],
        out_specs=pl.BlockSpec((4, nrows), lambda j: (0, 0)),
        out_shape=jax.ShapeDtypeStruct((4, nrows), jnp.float32),
        scratch_shapes=[pltpu.VMEM((1, nrows), jnp.float32)] * 4,
        compiler_params=pltpu.CompilerParams(dimension_semantics=("arbitrary",)),
    )(rows_t, local_targets, weight_t)


def body(hidden, gain, head_weight, targets, short_lengths, owner):
    own_rows, features = hidden.shape
    dp_pos = lax.axis_index("dp")
    dp_count = lax.axis_size("dp")
    tensor_pos = lax.axis_index("tensor")
    tensor_count = lax.axis_size("tensor")
    offset = tensor_pos * head_weight.shape[1]
    values = hidden.astype(jnp.float32)
    normed = (
        values * lax.rsqrt(jnp.mean(values * values, axis=1, keepdims=True) + 1e-06) * gain
    ).astype(jnp.bfloat16)

    digits = jnp.stack(
        [targets % DIGIT, (targets // DIGIT) % DIGIT, targets // (DIGIT * DIGIT)], axis=1
    ).astype(jnp.bfloat16)
    packed = jnp.concatenate(
        [normed, digits, jnp.zeros((own_rows, PAD_COLS - 3), jnp.bfloat16)], axis=1
    )
    gathered = lax.all_gather(packed, "tensor", axis=0, tiled=True)
    got = gathered[:, features:features + 3].astype(jnp.int32)
    rows_targets = got[:, 0] + DIGIT * got[:, 1] + (DIGIT * DIGIT) * got[:, 2]

    stats = fused_stats(gathered[:, :features].T, (rows_targets - offset)[None, :], head_weight.T)
    group_rows = stats.shape[1]
    devices = dp_count * tensor_count
    sent = jnp.broadcast_to(stats[None], (devices,) + stats.shape)
    everything = lax.all_to_all(sent, ("dp", "tensor"), 0, 0, tiled=True)
    everything = everything.reshape(dp_count, tensor_count, 4, group_rows)
    tops = everything[:, :, 0]
    joint = jnp.max(tops, axis=1)
    factor = jnp.exp(tops - joint[:, None, :])
    totals = everything[:, :, 1]
    row_total = jnp.sum(totals * factor, axis=1)
    spread = jnp.sum(factor * (everything[:, :, 2] + totals * (tops - joint[:, None, :])), axis=1)
    picked = jnp.sum(everything[:, :, 3], axis=1)
    total_rows = dp_count * group_rows
    row_top = joint.reshape(total_rows)
    row_total = row_total.reshape(total_rows)
    spread = spread.reshape(total_rows)
    picked = picked.reshape(total_rows)

    log_total = jnp.log(row_total)
    logprob = picked - row_top - log_total
    entropy = log_total - spread / row_total
    short_count = short_lengths.shape[0]
    long_len = total_rows - short_count * SLOT
    row_ids = lax.iota(jnp.int32, total_rows)
    past_long = row_ids - long_len
    sequence = jnp.where(row_ids < long_len, 0, 1 + past_long // SLOT)
    slot_pos = past_long % SLOT
    seq_lengths = jnp.concatenate([jnp.full((1,), long_len, jnp.int32), short_lengths])
    member = sequence[:, None] == lax.iota(jnp.int32, short_count + 1)[None, :]
    row_length = jnp.sum(jnp.where(member, seq_lengths[None, :], 0), axis=1)
    is_live = (row_ids < long_len) | (slot_pos < row_length)
    logprob = jnp.where(is_live, logprob, jnp.float32(0.0))
    entropy = jnp.where(is_live, entropy, jnp.float32(0.0))
    seq_sums = jnp.stack(
        [
            jnp.sum(jnp.where(member, logprob[:, None], jnp.float32(0.0)), axis=0),
            jnp.sum(jnp.where(member, entropy[:, None], jnp.float32(0.0)), axis=0),
        ]
    )
    seq_means = seq_sums / seq_lengths.astype(jnp.float32)[None, :]
    is_owner = owner == dp_pos
    seq_scores = jnp.where(is_owner[None, :], seq_means, jnp.float32(0.0))[None, :, :]
    start = (dp_pos * tensor_count + tensor_pos) * own_rows
    own_logprob = lax.dynamic_slice_in_dim(logprob, start, own_rows)
    own_entropy = lax.dynamic_slice_in_dim(entropy, start, own_rows)
    return (own_logprob, own_entropy, seq_scores)


def solution(mesh):
    return jax.shard_map(
        body,
        mesh=mesh,
        in_specs=(P(("dp", "tensor"), None), P(), P(None, "tensor"), P(("dp", "tensor")), P(), P()),
        out_specs=(P(("dp", "tensor")), P(("dp", "tensor")), P("dp", None, None)),
        check_vma=False,
    )
```

```python
import jax
import jax.numpy as jnp
from jax import lax
from jax.sharding import PartitionSpec as P

SLOT = 64
DIGIT = 256
PAD_COLS = 128


def local_stats(normed_rows, target_rows, weight, offset):
    logits = jnp.dot(normed_rows, weight, preferred_element_type=jnp.float32)
    row_top = jnp.max(logits, axis=1)
    shifted = logits - row_top[:, None]
    weights_exp = jnp.exp(shifted)
    row_total = jnp.sum(weights_exp, axis=1)
    spread = jnp.sum(weights_exp * shifted, axis=1)
    columns = lax.iota(jnp.int32, weight.shape[1]) + offset
    is_target = target_rows[:, None] == columns[None, :]
    picked = jnp.sum(jnp.where(is_target, logits, jnp.float32(0.0)), axis=1)
    return jnp.stack([row_top, row_total, spread, picked])


def body(hidden, gain, head_weight, targets, short_lengths, owner):
    own_rows, features = hidden.shape
    dp_pos = lax.axis_index("dp")
    dp_count = lax.axis_size("dp")
    tensor_pos = lax.axis_index("tensor")
    tensor_count = lax.axis_size("tensor")
    offset = tensor_pos * head_weight.shape[1]
    values = hidden.astype(jnp.float32)
    normed = (
        values * lax.rsqrt(jnp.mean(values * values, axis=1, keepdims=True) + 1e-06) * gain
    ).astype(jnp.bfloat16)

    place = lax.broadcasted_iota(jnp.int32, (own_rows, PAD_COLS), 1)
    scale = jnp.where(place == 0, 1, jnp.where(place == 1, DIGIT, DIGIT * DIGIT))
    digits = jnp.where(place < 3, (targets[:, None] // scale) % DIGIT, 0).astype(jnp.bfloat16)
    packed = jnp.concatenate([normed, digits], axis=1)
    gathered = lax.all_gather(packed, "tensor", axis=0, tiled=True)
    rows_normed = gathered[:, :features]
    got = gathered[:, features:features + 3].astype(jnp.int32)
    rows_targets = got[:, 0] + DIGIT * got[:, 1] + (DIGIT * DIGIT) * got[:, 2]

    stats = local_stats(rows_normed, rows_targets, head_weight, offset)
    group_rows = stats.shape[1]
    devices = dp_count * tensor_count
    sent = jnp.broadcast_to(stats[None], (devices,) + stats.shape)
    everything = lax.all_to_all(sent, ("dp", "tensor"), 0, 0, tiled=True)
    everything = everything.reshape(dp_count, tensor_count, 4, group_rows)
    tops = everything[:, :, 0]
    joint = jnp.max(tops, axis=1)
    factor = jnp.exp(tops - joint[:, None, :])
    totals = everything[:, :, 1]
    row_total = jnp.sum(totals * factor, axis=1)
    spread = jnp.sum(factor * (everything[:, :, 2] + totals * (tops - joint[:, None, :])), axis=1)
    picked = jnp.sum(everything[:, :, 3], axis=1)
    total_rows = dp_count * group_rows
    row_top = joint.reshape(total_rows)
    row_total = row_total.reshape(total_rows)
    spread = spread.reshape(total_rows)
    picked = picked.reshape(total_rows)

    log_total = jnp.log(row_total)
    logprob = picked - row_top - log_total
    entropy = log_total - spread / row_total
    short_count = short_lengths.shape[0]
    long_len = total_rows - short_count * SLOT
    row_ids = lax.iota(jnp.int32, total_rows)
    past_long = row_ids - long_len
    sequence = jnp.where(row_ids < long_len, 0, 1 + past_long // SLOT)
    slot_pos = past_long % SLOT
    seq_lengths = jnp.concatenate([jnp.full((1,), long_len, jnp.int32), short_lengths])
    member = sequence[:, None] == lax.iota(jnp.int32, short_count + 1)[None, :]
    row_length = jnp.sum(jnp.where(member, seq_lengths[None, :], 0), axis=1)
    is_live = (row_ids < long_len) | (slot_pos < row_length)
    logprob = jnp.where(is_live, logprob, jnp.float32(0.0))
    entropy = jnp.where(is_live, entropy, jnp.float32(0.0))
    seq_sums = jnp.stack(
        [
            jnp.sum(jnp.where(member, logprob[:, None], jnp.float32(0.0)), axis=0),
            jnp.sum(jnp.where(member, entropy[:, None], jnp.float32(0.0)), axis=0),
        ]
    )
    seq_means = seq_sums / seq_lengths.astype(jnp.float32)[None, :]
    is_owner = owner == dp_pos
    seq_scores = jnp.where(is_owner[None, :], seq_means, jnp.float32(0.0))[None, :, :]
    me = dp_pos * tensor_count + tensor_pos
    mine = (lax.iota(jnp.int32, devices) == me)[:, None]
    own_logprob = jnp.sum(jnp.where(mine, logprob.reshape(devices, own_rows), 0.0), axis=0)
    own_entropy = jnp.sum(jnp.where(mine, entropy.reshape(devices, own_rows), 0.0), axis=0)
    return (own_logprob, own_entropy, seq_scores)


def solution(mesh):
    return jax.shard_map(
        body,
        mesh=mesh,
        in_specs=(P(("dp", "tensor"), None), P(), P(None, "tensor"), P(("dp", "tensor")), P(), P()),
        out_specs=(P(("dp", "tensor")), P(("dp", "tensor")), P("dp", None, None)),
        check_vma=False,
    )
```

```python
import jax
import jax.numpy as jnp
from jax import lax
from jax.experimental import pallas as pl
from jax.experimental.pallas import tpu as pltpu
from jax.sharding import PartitionSpec as P

SLOT = 64
DIGIT = 256
PAD_COLS = 128


def pack_kernel(tgt_ref, hidden_ref, gain_ref, o_ref):
    rows, features = hidden_ref.shape
    values = hidden_ref[...].astype(jnp.float32)
    scale = lax.rsqrt(jnp.sum(values * values, axis=1, keepdims=True) / features + 1e-06)
    o_ref[:, :features] = (values * scale * gain_ref[...]).astype(jnp.bfloat16)
    place = lax.broadcasted_iota(jnp.int32, (rows, PAD_COLS), 1)
    row = lax.broadcasted_iota(jnp.int32, (rows, PAD_COLS), 0)
    target = jnp.zeros((rows, PAD_COLS), jnp.int32)
    for r in range(rows):
        target = jnp.where(row == r, tgt_ref[r], target)
    digit = jnp.where(place == 1, target // DIGIT, jnp.where(place == 2, target // (DIGIT * DIGIT), target))
    digit = jnp.where(place < 3, digit % DIGIT, 0)
    o_ref[:, features:] = digit.astype(jnp.float32).astype(jnp.bfloat16)


def pack_rows(hidden, gain, targets):
    rows, features = hidden.shape
    return pl.pallas_call(
        pack_kernel,
        in_specs=[
            pl.BlockSpec(memory_space=pltpu.SMEM),
            pl.BlockSpec((rows, features), lambda: (0, 0)),
            pl.BlockSpec((1, features), lambda: (0, 0)),
        ],
        out_specs=pl.BlockSpec((rows, features + PAD_COLS), lambda: (0, 0)),
        out_shape=jax.ShapeDtypeStruct((rows, features + PAD_COLS), jnp.bfloat16),
    )(targets, hidden, gain.reshape(1, features))


def local_stats(normed_rows, target_rows, weight, offset):
    logits = jnp.dot(normed_rows, weight, preferred_element_type=jnp.float32)
    row_top = jnp.max(logits, axis=1)
    shifted = logits - row_top[:, None]
    weights_exp = jnp.exp(shifted)
    row_total = jnp.sum(weights_exp, axis=1)
    spread = jnp.sum(weights_exp * shifted, axis=1)
    columns = lax.iota(jnp.int32, weight.shape[1]) + offset
    is_target = target_rows[:, None] == columns[None, :]
    picked = jnp.sum(jnp.where(is_target, logits, jnp.float32(0.0)), axis=1)
    return jnp.stack([row_top, row_total, spread, picked])


def body(hidden, gain, head_weight, targets, short_lengths, owner):
    own_rows, features = hidden.shape
    dp_pos = lax.axis_index("dp")
    dp_count = lax.axis_size("dp")
    tensor_pos = lax.axis_index("tensor")
    tensor_count = lax.axis_size("tensor")
    offset = tensor_pos * head_weight.shape[1]
    packed = pack_rows(hidden, gain, targets)
    gathered = lax.all_gather(packed, "tensor", axis=0, tiled=True)
    rows_normed = gathered[:, :features]
    got = gathered[:, features:features + 3].astype(jnp.int32)
    rows_targets = got[:, 0] + DIGIT * got[:, 1] + (DIGIT * DIGIT) * got[:, 2]

    stats = local_stats(rows_normed, rows_targets, head_weight, offset)
    group_rows = stats.shape[1]
    devices = dp_count * tensor_count
    sent = jnp.broadcast_to(stats[None], (devices,) + stats.shape)
    everything = lax.all_to_all(sent, ("dp", "tensor"), 0, 0, tiled=True)
    everything = everything.reshape(dp_count, tensor_count, 4, group_rows)
    tops = everything[:, :, 0]
    joint = jnp.max(tops, axis=1)
    factor = jnp.exp(tops - joint[:, None, :])
    totals = everything[:, :, 1]
    row_total = jnp.sum(totals * factor, axis=1)
    spread = jnp.sum(factor * (everything[:, :, 2] + totals * (tops - joint[:, None, :])), axis=1)
    picked = jnp.sum(everything[:, :, 3], axis=1)
    total_rows = dp_count * group_rows
    row_top = joint.reshape(total_rows)
    row_total = row_total.reshape(total_rows)
    spread = spread.reshape(total_rows)
    picked = picked.reshape(total_rows)

    log_total = jnp.log(row_total)
    logprob = picked - row_top - log_total
    entropy = log_total - spread / row_total
    short_count = short_lengths.shape[0]
    long_len = total_rows - short_count * SLOT
    row_ids = lax.iota(jnp.int32, total_rows)
    past_long = row_ids - long_len
    sequence = jnp.where(row_ids < long_len, 0, 1 + past_long // SLOT)
    slot_pos = past_long % SLOT
    seq_lengths = jnp.concatenate([jnp.full((1,), long_len, jnp.int32), short_lengths])
    member = sequence[:, None] == lax.iota(jnp.int32, short_count + 1)[None, :]
    row_length = jnp.sum(jnp.where(member, seq_lengths[None, :], 0), axis=1)
    is_live = (row_ids < long_len) | (slot_pos < row_length)
    logprob = jnp.where(is_live, logprob, jnp.float32(0.0))
    entropy = jnp.where(is_live, entropy, jnp.float32(0.0))
    seq_sums = jnp.stack(
        [
            jnp.sum(jnp.where(member, logprob[:, None], jnp.float32(0.0)), axis=0),
            jnp.sum(jnp.where(member, entropy[:, None], jnp.float32(0.0)), axis=0),
        ]
    )
    seq_means = seq_sums / seq_lengths.astype(jnp.float32)[None, :]
    is_owner = owner == dp_pos
    seq_scores = jnp.where(is_owner[None, :], seq_means, jnp.float32(0.0))[None, :, :]
    me = dp_pos * tensor_count + tensor_pos
    mine = (lax.iota(jnp.int32, devices) == me)[:, None]
    own_logprob = jnp.sum(jnp.where(mine, logprob.reshape(devices, own_rows), 0.0), axis=0)
    own_entropy = jnp.sum(jnp.where(mine, entropy.reshape(devices, own_rows), 0.0), axis=0)
    return (own_logprob, own_entropy, seq_scores)


def solution(mesh):
    return jax.shard_map(
        body,
        mesh=mesh,
        in_specs=(P(("dp", "tensor"), None), P(), P(None, "tensor"), P(("dp", "tensor")), P(), P()),
        out_specs=(P(("dp", "tensor")), P(("dp", "tensor")), P("dp", None, None)),
        check_vma=False,
    )
```

```python
import functools

import jax
import jax.numpy as jnp
from jax import lax
from jax.experimental import pallas as pl
from jax.experimental.pallas import tpu as pltpu
from jax.sharding import PartitionSpec as P

SLOT = 64
DIGIT = 256
PAD_COLS = 128


def pack_kernel(tgt_ref, hidden_ref, gain_ref, o_ref):
    rows, features = hidden_ref.shape
    values = hidden_ref[...].astype(jnp.float32)
    scale = lax.rsqrt(jnp.sum(values * values, axis=1, keepdims=True) / features + 1e-06)
    o_ref[:, :features] = (values * scale * gain_ref[...]).astype(jnp.bfloat16)
    place = lax.broadcasted_iota(jnp.int32, (rows, PAD_COLS), 1)
    row = lax.broadcasted_iota(jnp.int32, (rows, PAD_COLS), 0)
    target = jnp.zeros((rows, PAD_COLS), jnp.int32)
    for r in range(rows):
        target = jnp.where(row == r, tgt_ref[r], target)
    digit = jnp.where(place == 1, target // DIGIT, jnp.where(place == 2, target // (DIGIT * DIGIT), target))
    digit = jnp.where(place < 3, digit % DIGIT, 0)
    o_ref[:, features:] = digit.astype(jnp.float32).astype(jnp.bfloat16)


def pack_rows(hidden, gain, targets):
    rows, features = hidden.shape
    return pl.pallas_call(
        pack_kernel,
        in_specs=[
            pl.BlockSpec(memory_space=pltpu.SMEM),
            pl.BlockSpec((rows, features), lambda: (0, 0)),
            pl.BlockSpec((1, features), lambda: (0, 0)),
        ],
        out_specs=pl.BlockSpec((rows, features + PAD_COLS), lambda: (0, 0)),
        out_shape=jax.ShapeDtypeStruct((rows, features + PAD_COLS), jnp.bfloat16),
    )(targets, hidden, gain.reshape(1, features))


def total_of(values):
    return jnp.sum(jnp.sum(values, axis=1, keepdims=True), axis=0, keepdims=True)


def exact_pick(values, onehot):
    high = values.astype(jnp.bfloat16)
    rest = values - high.astype(jnp.float32)
    mid = rest.astype(jnp.bfloat16)
    low = (rest - mid.astype(jnp.float32)).astype(jnp.bfloat16)
    total = jnp.zeros((values.shape[0], onehot.shape[1]), jnp.float32)
    for part in (high, mid, low):
        total = total + jnp.dot(part, onehot, preferred_element_type=jnp.float32)
    return total


def finish_kernel(lengths_ref, owner_ref, place_ref, stats_ref, lp_ref, en_ref, seq_ref, *, own_rows):
    _, groups, group_rows = stats_ref.shape
    short_count = lengths_ref.shape[0]
    total_rows = groups * group_rows
    long_len = total_rows - short_count * SLOT
    row_top = stats_ref[0]
    row_total = stats_ref[1]
    log_total = jnp.log(row_total)
    logprob = stats_ref[3] - row_top - log_total
    entropy = log_total - stats_ref[2] / row_total
    row_ids = (
        lax.broadcasted_iota(jnp.int32, (groups, group_rows), 0) * group_rows
        + lax.broadcasted_iota(jnp.int32, (groups, group_rows), 1)
    )
    live = row_ids < long_len
    col = lax.broadcasted_iota(jnp.int32, (2, short_count + 1), 1)
    kind = lax.broadcasted_iota(jnp.int32, (2, short_count + 1), 0)
    means = jnp.zeros((2, short_count + 1), jnp.float32)
    sums = (
        total_of(jnp.where(live, logprob, 0.0)),
        total_of(jnp.where(live, entropy, 0.0)),
    )
    length = jnp.float32(long_len)
    means = jnp.where((col == 0) & (kind == 0), sums[0] / length, means)
    means = jnp.where((col == 0) & (kind == 1), sums[1] / length, means)
    for s in range(short_count):
        begin = long_len + s * SLOT
        member = (row_ids >= begin) & (row_ids < begin + lengths_ref[s])
        live = live | member
        length = lengths_ref[s].astype(jnp.float32)
        lp_sum = total_of(jnp.where(member, logprob, 0.0))
        en_sum = total_of(jnp.where(member, entropy, 0.0))
        means = jnp.where((col == s + 1) & (kind == 0), lp_sum / length, means)
        means = jnp.where((col == s + 1) & (kind == 1), en_sum / length, means)
    dp_pos = place_ref[0]
    for s in range(short_count + 1):
        means = jnp.where((col == s) & (owner_ref[s] != dp_pos), 0.0, means)
    seq_ref[0] = means
    logprob = jnp.where(live, logprob, 0.0)
    entropy = jnp.where(live, entropy, 0.0)
    onehot = (
        lax.broadcasted_iota(jnp.int32, (group_rows, own_rows), 0)
        == lax.broadcasted_iota(jnp.int32, (group_rows, own_rows), 1) + place_ref[1] * own_rows
    ).astype(jnp.bfloat16)
    group = lax.broadcasted_iota(jnp.int32, (groups, 1), 0) == dp_pos
    lp_row = jnp.sum(jnp.where(group, logprob, 0.0), axis=0, keepdims=True)
    en_row = jnp.sum(jnp.where(group, entropy, 0.0), axis=0, keepdims=True)
    lp_ref[...] = exact_pick(lp_row, onehot)
    en_ref[...] = exact_pick(en_row, onehot)


def finish(stats, short_lengths, owner, place, own_rows):
    short_count = short_lengths.shape[0]
    vmem = pl.BlockSpec(memory_space=pltpu.VMEM)
    smem = pl.BlockSpec(memory_space=pltpu.SMEM)
    return pl.pallas_call(
        functools.partial(finish_kernel, own_rows=own_rows),
        in_specs=[smem, smem, smem, vmem],
        out_specs=[vmem, vmem, vmem],
        out_shape=[
            jax.ShapeDtypeStruct((1, own_rows), jnp.float32),
            jax.ShapeDtypeStruct((1, own_rows), jnp.float32),
            jax.ShapeDtypeStruct((1, 2, short_count + 1), jnp.float32),
        ],
    )(short_lengths, owner, place, stats)


def local_stats(normed_rows, target_rows, weight, offset):
    logits = jnp.dot(normed_rows, weight, preferred_element_type=jnp.float32)
    row_top = jnp.max(logits, axis=1)
    shifted = logits - row_top[:, None]
    weights_exp = jnp.exp(shifted)
    row_total = jnp.sum(weights_exp, axis=1)
    spread = jnp.sum(weights_exp * shifted, axis=1)
    columns = lax.iota(jnp.int32, weight.shape[1]) + offset
    is_target = target_rows[:, None] == columns[None, :]
    picked = jnp.sum(jnp.where(is_target, logits, jnp.float32(0.0)), axis=1)
    return jnp.stack([row_top, row_total, spread, picked])


def body(hidden, gain, head_weight, targets, short_lengths, owner):
    own_rows, features = hidden.shape
    dp_pos = lax.axis_index("dp")
    dp_count = lax.axis_size("dp")
    tensor_pos = lax.axis_index("tensor")
    tensor_count = lax.axis_size("tensor")
    offset = tensor_pos * head_weight.shape[1]
    packed = pack_rows(hidden, gain, targets)
    gathered = lax.all_gather(packed, "tensor", axis=0, tiled=True)
    rows_normed = gathered[:, :features]
    got = gathered[:, features:features + 3].astype(jnp.int32)
    rows_targets = got[:, 0] + DIGIT * got[:, 1] + (DIGIT * DIGIT) * got[:, 2]

    stats = local_stats(rows_normed, rows_targets, head_weight, offset)
    group_rows = stats.shape[1]
    devices = dp_count * tensor_count
    sent = jnp.broadcast_to(stats[None], (devices,) + stats.shape)
    everything = lax.all_to_all(sent, ("dp", "tensor"), 0, 0, tiled=True)
    everything = everything.reshape(dp_count, tensor_count, 4, group_rows)
    tops = everything[:, :, 0]
    joint = jnp.max(tops, axis=1)
    factor = jnp.exp(tops - joint[:, None, :])
    totals = everything[:, :, 1]
    row_total = jnp.sum(totals * factor, axis=1)
    spread = jnp.sum(factor * (everything[:, :, 2] + totals * (tops - joint[:, None, :])), axis=1)
    picked = jnp.sum(everything[:, :, 3], axis=1)
    row_top = joint

    place = jnp.stack([dp_pos, tensor_pos]).astype(jnp.int32)
    own_logprob, own_entropy, seq_scores = finish(
        jnp.stack([row_top, row_total, spread, picked]).reshape(4, dp_count, group_rows),
        short_lengths, owner, place, own_rows,
    )
    return (own_logprob.reshape(own_rows), own_entropy.reshape(own_rows), seq_scores)


def solution(mesh):
    return jax.shard_map(
        body,
        mesh=mesh,
        in_specs=(P(("dp", "tensor"), None), P(), P(None, "tensor"), P(("dp", "tensor")), P(), P()),
        out_specs=(P(("dp", "tensor")), P(("dp", "tensor")), P("dp", None, None)),
        check_vma=False,
    )
```

```python
import functools

import jax
import jax.numpy as jnp
from jax import lax
from jax.experimental import pallas as pl
from jax.experimental.pallas import tpu as pltpu
from jax.sharding import PartitionSpec as P

SLOT = 64
FLOOR = -1e30
DIGIT = 256
PAD_COLS = 128


def pack_kernel(tgt_ref, hidden_ref, gain_ref, o_ref):
    rows, features = hidden_ref.shape
    values = hidden_ref[...].astype(jnp.float32)
    scale = lax.rsqrt(jnp.sum(values * values, axis=1, keepdims=True) / features + 1e-06)
    o_ref[:, :features] = (values * scale * gain_ref[...]).astype(jnp.bfloat16)
    place = lax.broadcasted_iota(jnp.int32, (rows, PAD_COLS), 1)
    row = lax.broadcasted_iota(jnp.int32, (rows, PAD_COLS), 0)
    target = jnp.zeros((rows, PAD_COLS), jnp.int32)
    for r in range(rows):
        target = jnp.where(row == r, tgt_ref[r], target)
    digit = jnp.where(place == 1, target // DIGIT, jnp.where(place == 2, target // (DIGIT * DIGIT), target))
    digit = jnp.where(place < 3, digit % DIGIT, 0)
    o_ref[:, features:] = digit.astype(jnp.float32).astype(jnp.bfloat16)


def pack_rows(hidden, gain, targets):
    rows, features = hidden.shape
    return pl.pallas_call(
        pack_kernel,
        in_specs=[
            pl.BlockSpec(memory_space=pltpu.SMEM),
            pl.BlockSpec((rows, features), lambda: (0, 0)),
            pl.BlockSpec((1, features), lambda: (0, 0)),
        ],
        out_specs=pl.BlockSpec((rows, features + PAD_COLS), lambda: (0, 0)),
        out_shape=jax.ShapeDtypeStruct((rows, features + PAD_COLS), jnp.bfloat16),
    )(targets, hidden, gain.reshape(1, features))


def total_of(values):
    return jnp.sum(jnp.sum(values, axis=1, keepdims=True), axis=0, keepdims=True)


def exact_pick(values, onehot):
    high = values.astype(jnp.bfloat16)
    rest = values - high.astype(jnp.float32)
    mid = rest.astype(jnp.bfloat16)
    low = (rest - mid.astype(jnp.float32)).astype(jnp.bfloat16)
    total = jnp.zeros((values.shape[0], onehot.shape[1]), jnp.float32)
    for part in (high, mid, low):
        total = total + jnp.dot(part, onehot, preferred_element_type=jnp.float32)
    return total


def combine_group(stats_ref, first, count):
    group_rows = stats_ref.shape[2]

    def step(t, carry):
        top, total, spread, picked = carry
        block = stats_ref[first + t]
        new_top = jnp.maximum(top, block[0:1])
        keep = jnp.exp(top - new_top)
        take = jnp.exp(block[0:1] - new_top)
        spread = keep * (spread + total * (top - new_top)) + take * (
            block[2:3] + block[1:2] * (block[0:1] - new_top)
        )
        total = total * keep + block[1:2] * take
        return new_top, total, spread, picked + block[3:4]

    zero = jnp.zeros((1, group_rows), jnp.float32)
    return lax.fori_loop(0, count, step, (jnp.full((1, group_rows), FLOOR, jnp.float32), zero, zero, zero))


def finish_kernel(lengths_ref, owner_ref, place_ref, stats_ref, lp_ref, en_ref, seq_ref, *, own_rows, groups):
    devices, _, group_rows = stats_ref.shape
    per_group = devices // groups
    short_count = lengths_ref.shape[0]
    total_rows = groups * group_rows
    long_len = total_rows - short_count * SLOT
    parts = [combine_group(stats_ref, d * per_group, per_group) for d in range(groups)]
    row_top, row_total, spread, picked = (
        jnp.concatenate([part[k] for part in parts], axis=0) for k in range(4)
    )
    log_total = jnp.log(row_total)
    logprob = picked - row_top - log_total
    entropy = log_total - spread / row_total
    row_ids = (
        lax.broadcasted_iota(jnp.int32, (groups, group_rows), 0) * group_rows
        + lax.broadcasted_iota(jnp.int32, (groups, group_rows), 1)
    )
    live = row_ids < long_len
    col = lax.broadcasted_iota(jnp.int32, (2, short_count + 1), 1)
    kind = lax.broadcasted_iota(jnp.int32, (2, short_count + 1), 0)
    means = jnp.zeros((2, short_count + 1), jnp.float32)
    sums = (
        total_of(jnp.where(live, logprob, 0.0)),
        total_of(jnp.where(live, entropy, 0.0)),
    )
    length = jnp.float32(long_len)
    means = jnp.where((col == 0) & (kind == 0), sums[0] / length, means)
    means = jnp.where((col == 0) & (kind == 1), sums[1] / length, means)
    for s in range(short_count):
        begin = long_len + s * SLOT
        member = (row_ids >= begin) & (row_ids < begin + lengths_ref[s])
        live = live | member
        length = lengths_ref[s].astype(jnp.float32)
        lp_sum = total_of(jnp.where(member, logprob, 0.0))
        en_sum = total_of(jnp.where(member, entropy, 0.0))
        means = jnp.where((col == s + 1) & (kind == 0), lp_sum / length, means)
        means = jnp.where((col == s + 1) & (kind == 1), en_sum / length, means)
    dp_pos = place_ref[0]
    for s in range(short_count + 1):
        means = jnp.where((col == s) & (owner_ref[s] != dp_pos), 0.0, means)
    seq_ref[0] = means
    logprob = jnp.where(live, logprob, 0.0)
    entropy = jnp.where(live, entropy, 0.0)
    onehot = (
        lax.broadcasted_iota(jnp.int32, (group_rows, own_rows), 0)
        == lax.broadcasted_iota(jnp.int32, (group_rows, own_rows), 1) + place_ref[1] * own_rows
    ).astype(jnp.bfloat16)
    group = lax.broadcasted_iota(jnp.int32, (groups, 1), 0) == dp_pos
    lp_row = jnp.sum(jnp.where(group, logprob, 0.0), axis=0, keepdims=True)
    en_row = jnp.sum(jnp.where(group, entropy, 0.0), axis=0, keepdims=True)
    lp_ref[...] = exact_pick(lp_row, onehot)
    en_ref[...] = exact_pick(en_row, onehot)


def finish(stats, short_lengths, owner, place, own_rows, groups):
    short_count = short_lengths.shape[0]
    vmem = pl.BlockSpec(memory_space=pltpu.VMEM)
    smem = pl.BlockSpec(memory_space=pltpu.SMEM)
    return pl.pallas_call(
        functools.partial(finish_kernel, own_rows=own_rows, groups=groups),
        in_specs=[smem, smem, smem, vmem],
        out_specs=[vmem, vmem, vmem],
        out_shape=[
            jax.ShapeDtypeStruct((1, own_rows), jnp.float32),
            jax.ShapeDtypeStruct((1, own_rows), jnp.float32),
            jax.ShapeDtypeStruct((1, 2, short_count + 1), jnp.float32),
        ],
    )(short_lengths, owner, place, stats)


def local_stats(normed_rows, target_rows, weight, offset):
    logits = jnp.dot(normed_rows, weight, preferred_element_type=jnp.float32)
    row_top = jnp.max(logits, axis=1)
    shifted = logits - row_top[:, None]
    weights_exp = jnp.exp(shifted)
    row_total = jnp.sum(weights_exp, axis=1)
    spread = jnp.sum(weights_exp * shifted, axis=1)
    columns = lax.iota(jnp.int32, weight.shape[1]) + offset
    is_target = target_rows[:, None] == columns[None, :]
    picked = jnp.sum(jnp.where(is_target, logits, jnp.float32(0.0)), axis=1)
    return jnp.stack([row_top, row_total, spread, picked])


def body(hidden, gain, head_weight, targets, short_lengths, owner):
    own_rows, features = hidden.shape
    dp_pos = lax.axis_index("dp")
    dp_count = lax.axis_size("dp")
    tensor_pos = lax.axis_index("tensor")
    tensor_count = lax.axis_size("tensor")
    offset = tensor_pos * head_weight.shape[1]
    packed = pack_rows(hidden, gain, targets)
    gathered = lax.all_gather(packed, "tensor", axis=0, tiled=True)
    rows_normed = gathered[:, :features]
    got = gathered[:, features:features + 3].astype(jnp.int32)
    rows_targets = got[:, 0] + DIGIT * got[:, 1] + (DIGIT * DIGIT) * got[:, 2]

    stats = local_stats(rows_normed, rows_targets, head_weight, offset)
    group_rows = stats.shape[1]
    devices = dp_count * tensor_count
    sent = jnp.broadcast_to(stats[None], (devices,) + stats.shape)
    everything = lax.all_to_all(sent, ("dp", "tensor"), 0, 0, tiled=True)
    place = jnp.stack([dp_pos, tensor_pos]).astype(jnp.int32)
    own_logprob, own_entropy, seq_scores = finish(
        everything, short_lengths, owner, place, own_rows, dp_count,
    )
    return (own_logprob.reshape(own_rows), own_entropy.reshape(own_rows), seq_scores)


def solution(mesh):
    return jax.shard_map(
        body,
        mesh=mesh,
        in_specs=(P(("dp", "tensor"), None), P(), P(None, "tensor"), P(("dp", "tensor")), P(), P()),
        out_specs=(P(("dp", "tensor")), P(("dp", "tensor")), P("dp", None, None)),
        check_vma=False,
    )
```

```python
import jax
import jax.numpy as jnp
from jax import lax
from jax.experimental import pallas as pl
from jax.experimental.pallas import tpu as pltpu
from jax.sharding import PartitionSpec as P

SLOT = 64
DIGIT = 256
PAD_COLS = 128
LOW_GROUP = 4


def pack_kernel(tgt_ref, hidden_ref, gain_ref, o_ref):
    rows, features = hidden_ref.shape
    values = hidden_ref[...].astype(jnp.float32)
    scale = lax.rsqrt(jnp.sum(values * values, axis=1, keepdims=True) / features + 1e-06)
    o_ref[:, :features] = (values * scale * gain_ref[...]).astype(jnp.bfloat16)
    place = lax.broadcasted_iota(jnp.int32, (rows, PAD_COLS), 1)
    row = lax.broadcasted_iota(jnp.int32, (rows, PAD_COLS), 0)
    target = jnp.zeros((rows, PAD_COLS), jnp.int32)
    for r in range(rows):
        target = jnp.where(row == r, tgt_ref[r], target)
    digit = jnp.where(place == 1, target // DIGIT, jnp.where(place == 2, target // (DIGIT * DIGIT), target))
    digit = jnp.where(place < 3, digit % DIGIT, 0)
    o_ref[:, features:] = digit.astype(jnp.float32).astype(jnp.bfloat16)


def pack_rows(hidden, gain, targets):
    rows, features = hidden.shape
    return pl.pallas_call(
        pack_kernel,
        in_specs=[
            pl.BlockSpec(memory_space=pltpu.SMEM),
            pl.BlockSpec((rows, features), lambda: (0, 0)),
            pl.BlockSpec((1, features), lambda: (0, 0)),
        ],
        out_specs=pl.BlockSpec((rows, features + PAD_COLS), lambda: (0, 0)),
        out_shape=jax.ShapeDtypeStruct((rows, features + PAD_COLS), jnp.bfloat16),
    )(targets, hidden, gain.reshape(1, features))


def gather_rows(packed, tensor_pos, tensor_count):
    high = tensor_count // LOW_GROUP
    if tensor_count % LOW_GROUP or high & (high - 1) or high == 1:
        return lax.all_gather(packed, "tensor", axis=0, tiled=True), lambda stats: stats
    blocks = [packed] + [
        lax.ppermute(packed, "tensor", [(i, i ^ (k * LOW_GROUP)) for i in range(tensor_count)])
        for k in range(1, high)
    ]
    groups = [[h * LOW_GROUP + low for low in range(LOW_GROUP)] for h in range(high)]
    gathered = lax.all_gather(
        jnp.concatenate(blocks, axis=0), "tensor", axis=0, tiled=True, axis_index_groups=groups
    )
    own_rows = packed.shape[0]
    order = lax.iota(jnp.int32, high) ^ (tensor_pos // LOW_GROUP)

    def restore(stats):
        stats = stats.reshape(stats.shape[0], LOW_GROUP, high, own_rows)
        stats = jnp.take(stats, order, axis=2)
        return stats.transpose(0, 2, 1, 3).reshape(stats.shape[0], tensor_count * own_rows)

    return gathered, restore


def local_stats(normed_rows, target_rows, weight, offset):
    logits = jnp.dot(normed_rows, weight, preferred_element_type=jnp.float32)
    row_top = jnp.max(logits, axis=1)
    shifted = logits - row_top[:, None]
    weights_exp = jnp.exp(shifted)
    row_total = jnp.sum(weights_exp, axis=1)
    spread = jnp.sum(weights_exp * shifted, axis=1)
    columns = lax.iota(jnp.int32, weight.shape[1]) + offset
    is_target = target_rows[:, None] == columns[None, :]
    picked = jnp.sum(jnp.where(is_target, logits, jnp.float32(0.0)), axis=1)
    return jnp.stack([row_top, row_total, spread, picked])


def body(hidden, gain, head_weight, targets, short_lengths, owner):
    own_rows, features = hidden.shape
    dp_pos = lax.axis_index("dp")
    dp_count = lax.axis_size("dp")
    tensor_pos = lax.axis_index("tensor")
    tensor_count = lax.axis_size("tensor")
    offset = tensor_pos * head_weight.shape[1]
    packed = pack_rows(hidden, gain, targets)
    gathered, restore = gather_rows(packed, tensor_pos, tensor_count)
    rows_normed = gathered[:, :features]
    got = gathered[:, features:features + 3].astype(jnp.int32)
    rows_targets = got[:, 0] + DIGIT * got[:, 1] + (DIGIT * DIGIT) * got[:, 2]

    stats = restore(local_stats(rows_normed, rows_targets, head_weight, offset))
    group_rows = stats.shape[1]
    devices = dp_count * tensor_count
    sent = jnp.broadcast_to(stats[None], (devices,) + stats.shape)
    everything = lax.all_to_all(sent, ("dp", "tensor"), 0, 0, tiled=True)
    everything = everything.reshape(dp_count, tensor_count, 4, group_rows)
    tops = everything[:, :, 0]
    joint = jnp.max(tops, axis=1)
    factor = jnp.exp(tops - joint[:, None, :])
    totals = everything[:, :, 1]
    row_total = jnp.sum(totals * factor, axis=1)
    spread = jnp.sum(factor * (everything[:, :, 2] + totals * (tops - joint[:, None, :])), axis=1)
    picked = jnp.sum(everything[:, :, 3], axis=1)
    total_rows = dp_count * group_rows
    row_top = joint.reshape(total_rows)
    row_total = row_total.reshape(total_rows)
    spread = spread.reshape(total_rows)
    picked = picked.reshape(total_rows)

    log_total = jnp.log(row_total)
    logprob = picked - row_top - log_total
    entropy = log_total - spread / row_total
    short_count = short_lengths.shape[0]
    long_len = total_rows - short_count * SLOT
    row_ids = lax.iota(jnp.int32, total_rows)
    past_long = row_ids - long_len
    sequence = jnp.where(row_ids < long_len, 0, 1 + past_long // SLOT)
    slot_pos = past_long % SLOT
    seq_lengths = jnp.concatenate([jnp.full((1,), long_len, jnp.int32), short_lengths])
    member = sequence[:, None] == lax.iota(jnp.int32, short_count + 1)[None, :]
    row_length = jnp.sum(jnp.where(member, seq_lengths[None, :], 0), axis=1)
    is_live = (row_ids < long_len) | (slot_pos < row_length)
    logprob = jnp.where(is_live, logprob, jnp.float32(0.0))
    entropy = jnp.where(is_live, entropy, jnp.float32(0.0))
    seq_sums = jnp.stack(
        [
            jnp.sum(jnp.where(member, logprob[:, None], jnp.float32(0.0)), axis=0),
            jnp.sum(jnp.where(member, entropy[:, None], jnp.float32(0.0)), axis=0),
        ]
    )
    seq_means = seq_sums / seq_lengths.astype(jnp.float32)[None, :]
    is_owner = owner == dp_pos
    seq_scores = jnp.where(is_owner[None, :], seq_means, jnp.float32(0.0))[None, :, :]
    me = dp_pos * tensor_count + tensor_pos
    mine = (lax.iota(jnp.int32, devices) == me)[:, None]
    own_logprob = jnp.sum(jnp.where(mine, logprob.reshape(devices, own_rows), 0.0), axis=0)
    own_entropy = jnp.sum(jnp.where(mine, entropy.reshape(devices, own_rows), 0.0), axis=0)
    return (own_logprob, own_entropy, seq_scores)


def solution(mesh):
    return jax.shard_map(
        body,
        mesh=mesh,
        in_specs=(P(("dp", "tensor"), None), P(), P(None, "tensor"), P(("dp", "tensor")), P(), P()),
        out_specs=(P(("dp", "tensor")), P(("dp", "tensor")), P("dp", None, None)),
        check_vma=False,
    )
```

```python
import jax
import jax.numpy as jnp
from jax import lax
from jax.experimental import pallas as pl
from jax.experimental.pallas import tpu as pltpu
from jax.sharding import PartitionSpec as P

SLOT = 64
DIGIT = 256
PAD_COLS = 128
LOW_GROUP = 4
CHUNKS = 4


def pack_kernel(tgt_ref, hidden_ref, gain_ref, o_ref):
    rows, features = hidden_ref.shape
    values = hidden_ref[...].astype(jnp.float32)
    scale = lax.rsqrt(jnp.sum(values * values, axis=1, keepdims=True) / features + 1e-06)
    o_ref[:, :features] = (values * scale * gain_ref[...]).astype(jnp.bfloat16)
    place = lax.broadcasted_iota(jnp.int32, (rows, PAD_COLS), 1)
    row = lax.broadcasted_iota(jnp.int32, (rows, PAD_COLS), 0)
    target = jnp.zeros((rows, PAD_COLS), jnp.int32)
    for r in range(rows):
        target = jnp.where(row == r, tgt_ref[r], target)
    digit = jnp.where(place == 1, target // DIGIT, jnp.where(place == 2, target // (DIGIT * DIGIT), target))
    digit = jnp.where(place < 3, digit % DIGIT, 0)
    o_ref[:, features:] = digit.astype(jnp.float32).astype(jnp.bfloat16)


def pack_rows(hidden, gain, targets):
    rows, features = hidden.shape
    return pl.pallas_call(
        pack_kernel,
        in_specs=[
            pl.BlockSpec(memory_space=pltpu.SMEM),
            pl.BlockSpec((rows, features), lambda: (0, 0)),
            pl.BlockSpec((1, features), lambda: (0, 0)),
        ],
        out_specs=pl.BlockSpec((rows, features + PAD_COLS), lambda: (0, 0)),
        out_shape=jax.ShapeDtypeStruct((rows, features + PAD_COLS), jnp.bfloat16),
    )(targets, hidden, gain.reshape(1, features))


def gather_rows(packed, tensor_pos, tensor_count):
    high = tensor_count // LOW_GROUP
    if tensor_count % LOW_GROUP or high & (high - 1) or high == 1:
        return lax.all_gather(packed, "tensor", axis=0, tiled=True), lambda stats: stats
    blocks = [packed] + [
        lax.ppermute(packed, "tensor", [(i, i ^ (k * LOW_GROUP)) for i in range(tensor_count)])
        for k in range(1, high)
    ]
    groups = [[h * LOW_GROUP + low for low in range(LOW_GROUP)] for h in range(high)]
    gathered = lax.all_gather(
        jnp.concatenate(blocks, axis=0), "tensor", axis=0, tiled=True, axis_index_groups=groups
    )
    own_rows = packed.shape[0]
    order = lax.iota(jnp.int32, high) ^ (tensor_pos // LOW_GROUP)

    def restore(stats):
        stats = stats.reshape(stats.shape[0], LOW_GROUP, high, own_rows)
        stats = jnp.take(stats, order, axis=2)
        return stats.transpose(0, 2, 1, 3).reshape(stats.shape[0], tensor_count * own_rows)

    return gathered, restore


def chunk_stats(normed_rows, target_rows, weight, offset):
    logits = jnp.dot(normed_rows, weight, preferred_element_type=jnp.float32)
    row_top = jnp.max(logits, axis=1)
    shifted = logits - row_top[:, None]
    weights_exp = jnp.exp(shifted)
    row_total = jnp.sum(weights_exp, axis=1)
    spread = jnp.sum(weights_exp * shifted, axis=1)
    columns = lax.iota(jnp.int32, weight.shape[1]) + offset
    is_target = target_rows[:, None] == columns[None, :]
    picked = jnp.sum(jnp.where(is_target, logits, jnp.float32(0.0)), axis=1)
    return (row_top, row_total, spread, picked)


def local_stats(normed_rows, target_rows, weight, offset):
    width = weight.shape[1]
    chunks = CHUNKS if width % CHUNKS == 0 else 1
    step = width // chunks
    parts = [
        chunk_stats(normed_rows, target_rows, weight[:, c * step:(c + 1) * step], offset + c * step)
        for c in range(chunks)
    ]
    top = parts[0][0]
    for part in parts[1:]:
        top = jnp.maximum(top, part[0])
    total = jnp.zeros_like(top)
    spread = jnp.zeros_like(top)
    picked = jnp.zeros_like(top)
    for part in parts:
        factor = jnp.exp(part[0] - top)
        total = total + part[1] * factor
        spread = spread + factor * (part[2] + part[1] * (part[0] - top))
        picked = picked + part[3]
    return jnp.stack([top, total, spread, picked])


def body(hidden, gain, head_weight, targets, short_lengths, owner):
    own_rows, features = hidden.shape
    dp_pos = lax.axis_index("dp")
    dp_count = lax.axis_size("dp")
    tensor_pos = lax.axis_index("tensor")
    tensor_count = lax.axis_size("tensor")
    offset = tensor_pos * head_weight.shape[1]
    packed = pack_rows(hidden, gain, targets)
    gathered, restore = gather_rows(packed, tensor_pos, tensor_count)
    rows_normed = gathered[:, :features]
    got = gathered[:, features:features + 3].astype(jnp.int32)
    rows_targets = got[:, 0] + DIGIT * got[:, 1] + (DIGIT * DIGIT) * got[:, 2]

    stats = restore(local_stats(rows_normed, rows_targets, head_weight, offset))
    group_rows = stats.shape[1]
    devices = dp_count * tensor_count
    sent = jnp.broadcast_to(stats[None], (devices,) + stats.shape)
    everything = lax.all_to_all(sent, ("dp", "tensor"), 0, 0, tiled=True)
    everything = everything.reshape(dp_count, tensor_count, 4, group_rows)
    tops = everything[:, :, 0]
    joint = jnp.max(tops, axis=1)
    factor = jnp.exp(tops - joint[:, None, :])
    totals = everything[:, :, 1]
    row_total = jnp.sum(totals * factor, axis=1)
    spread = jnp.sum(factor * (everything[:, :, 2] + totals * (tops - joint[:, None, :])), axis=1)
    picked = jnp.sum(everything[:, :, 3], axis=1)
    total_rows = dp_count * group_rows
    row_top = joint.reshape(total_rows)
    row_total = row_total.reshape(total_rows)
    spread = spread.reshape(total_rows)
    picked = picked.reshape(total_rows)

    log_total = jnp.log(row_total)
    logprob = picked - row_top - log_total
    entropy = log_total - spread / row_total
    short_count = short_lengths.shape[0]
    long_len = total_rows - short_count * SLOT
    row_ids = lax.iota(jnp.int32, total_rows)
    past_long = row_ids - long_len
    sequence = jnp.where(row_ids < long_len, 0, 1 + past_long // SLOT)
    slot_pos = past_long % SLOT
    seq_lengths = jnp.concatenate([jnp.full((1,), long_len, jnp.int32), short_lengths])
    member = sequence[:, None] == lax.iota(jnp.int32, short_count + 1)[None, :]
    row_length = jnp.sum(jnp.where(member, seq_lengths[None, :], 0), axis=1)
    is_live = (row_ids < long_len) | (slot_pos < row_length)
    logprob = jnp.where(is_live, logprob, jnp.float32(0.0))
    entropy = jnp.where(is_live, entropy, jnp.float32(0.0))
    seq_sums = jnp.stack(
        [
            jnp.sum(jnp.where(member, logprob[:, None], jnp.float32(0.0)), axis=0),
            jnp.sum(jnp.where(member, entropy[:, None], jnp.float32(0.0)), axis=0),
        ]
    )
    seq_means = seq_sums / seq_lengths.astype(jnp.float32)[None, :]
    is_owner = owner == dp_pos
    seq_scores = jnp.where(is_owner[None, :], seq_means, jnp.float32(0.0))[None, :, :]
    me = dp_pos * tensor_count + tensor_pos
    mine = (lax.iota(jnp.int32, devices) == me)[:, None]
    own_logprob = jnp.sum(jnp.where(mine, logprob.reshape(devices, own_rows), 0.0), axis=0)
    own_entropy = jnp.sum(jnp.where(mine, entropy.reshape(devices, own_rows), 0.0), axis=0)
    return (own_logprob, own_entropy, seq_scores)


def solution(mesh):
    return jax.shard_map(
        body,
        mesh=mesh,
        in_specs=(P(("dp", "tensor"), None), P(), P(None, "tensor"), P(("dp", "tensor")), P(), P()),
        out_specs=(P(("dp", "tensor")), P(("dp", "tensor")), P("dp", None, None)),
        check_vma=False,
    )
```

```python
import jax
import jax.numpy as jnp
from jax import lax
from jax.experimental import pallas as pl
from jax.experimental.pallas import tpu as pltpu
from jax.sharding import PartitionSpec as P

SLOT = 64
DIGIT = 256
PAD_COLS = 128
LOW_GROUP = 4
CHUNKS = 4


def pack_kernel(tgt_ref, hidden_ref, gain_ref, o_ref):
    rows, features = hidden_ref.shape
    values = hidden_ref[...].astype(jnp.float32)
    scale = lax.rsqrt(jnp.sum(values * values, axis=1, keepdims=True) / features + 1e-06)
    o_ref[:, :features] = (values * scale * gain_ref[...]).astype(jnp.bfloat16)
    place = lax.broadcasted_iota(jnp.int32, (rows, PAD_COLS), 1)
    row = lax.broadcasted_iota(jnp.int32, (rows, PAD_COLS), 0)
    target = jnp.zeros((rows, PAD_COLS), jnp.int32)
    for r in range(rows):
        target = jnp.where(row == r, tgt_ref[r], target)
    digit = jnp.where(place == 1, target // DIGIT, jnp.where(place == 2, target // (DIGIT * DIGIT), target))
    digit = jnp.where(place < 3, digit % DIGIT, 0)
    o_ref[:, features:] = digit.astype(jnp.float32).astype(jnp.bfloat16)


def pack_rows(hidden, gain, targets):
    rows, features = hidden.shape
    return pl.pallas_call(
        pack_kernel,
        in_specs=[
            pl.BlockSpec(memory_space=pltpu.SMEM),
            pl.BlockSpec((rows, features), lambda: (0, 0)),
            pl.BlockSpec((1, features), lambda: (0, 0)),
        ],
        out_specs=pl.BlockSpec((rows, features + PAD_COLS), lambda: (0, 0)),
        out_shape=jax.ShapeDtypeStruct((rows, features + PAD_COLS), jnp.bfloat16),
    )(targets, hidden, gain.reshape(1, features))


def gather_rows(packed, tensor_pos, tensor_count):
    high = tensor_count // LOW_GROUP
    if tensor_count % LOW_GROUP or high & (high - 1) or high == 1:
        return lax.all_gather(packed, "tensor", axis=0, tiled=True), lambda stats: stats
    blocks = [packed] + [
        lax.ppermute(packed, "tensor", [(i, i ^ (k * LOW_GROUP)) for i in range(tensor_count)])
        for k in range(1, high)
    ]
    groups = [[h * LOW_GROUP + low for low in range(LOW_GROUP)] for h in range(high)]
    gathered = lax.all_gather(
        jnp.concatenate(blocks, axis=0), "tensor", axis=0, tiled=True, axis_index_groups=groups
    )
    own_rows = packed.shape[0]
    order = lax.iota(jnp.int32, high) ^ (tensor_pos // LOW_GROUP)

    def restore(stats):
        stats = stats.reshape(stats.shape[0], LOW_GROUP, high, own_rows)
        stats = jnp.take(stats, order, axis=2)
        return stats.transpose(0, 2, 1, 3).reshape(stats.shape[0], tensor_count * own_rows)

    return gathered, restore


def chunk_stats(normed_rows, target_rows, weight, offset):
    logits = jnp.dot(normed_rows, weight, preferred_element_type=jnp.float32)
    row_top = jnp.max(logits, axis=1)
    shifted = logits - row_top[:, None]
    weights_exp = jnp.exp(shifted)
    row_total = jnp.sum(weights_exp, axis=1)
    spread = jnp.sum(weights_exp * shifted, axis=1)
    columns = lax.iota(jnp.int32, weight.shape[1]) + offset
    is_target = target_rows[:, None] == columns[None, :]
    picked = jnp.sum(jnp.where(is_target, logits, jnp.float32(0.0)), axis=1)
    return (row_top, row_total, spread, picked)


def local_stats(normed_rows, target_rows, weight, offset):
    width = weight.shape[1]
    chunks = CHUNKS if width % CHUNKS == 0 else 1
    step = width // chunks
    parts = []
    for c in range(chunks):
        part = chunk_stats(normed_rows, target_rows, weight[:, c * step:(c + 1) * step], offset + c * step)
        part, normed_rows = lax.optimization_barrier((part, normed_rows))
        parts.append(part)
    top = parts[0][0]
    for part in parts[1:]:
        top = jnp.maximum(top, part[0])
    total = jnp.zeros_like(top)
    spread = jnp.zeros_like(top)
    picked = jnp.zeros_like(top)
    for part in parts:
        factor = jnp.exp(part[0] - top)
        total = total + part[1] * factor
        spread = spread + factor * (part[2] + part[1] * (part[0] - top))
        picked = picked + part[3]
    return jnp.stack([top, total, spread, picked])


def body(hidden, gain, head_weight, targets, short_lengths, owner):
    own_rows, features = hidden.shape
    dp_pos = lax.axis_index("dp")
    dp_count = lax.axis_size("dp")
    tensor_pos = lax.axis_index("tensor")
    tensor_count = lax.axis_size("tensor")
    offset = tensor_pos * head_weight.shape[1]
    packed = pack_rows(hidden, gain, targets)
    gathered, restore = gather_rows(packed, tensor_pos, tensor_count)
    rows_normed = gathered[:, :features]
    got = gathered[:, features:features + 3].astype(jnp.int32)
    rows_targets = got[:, 0] + DIGIT * got[:, 1] + (DIGIT * DIGIT) * got[:, 2]

    stats = restore(local_stats(rows_normed, rows_targets, head_weight, offset))
    group_rows = stats.shape[1]
    devices = dp_count * tensor_count
    sent = jnp.broadcast_to(stats[None], (devices,) + stats.shape)
    everything = lax.all_to_all(sent, ("dp", "tensor"), 0, 0, tiled=True)
    everything = everything.reshape(dp_count, tensor_count, 4, group_rows)
    tops = everything[:, :, 0]
    joint = jnp.max(tops, axis=1)
    factor = jnp.exp(tops - joint[:, None, :])
    totals = everything[:, :, 1]
    row_total = jnp.sum(totals * factor, axis=1)
    spread = jnp.sum(factor * (everything[:, :, 2] + totals * (tops - joint[:, None, :])), axis=1)
    picked = jnp.sum(everything[:, :, 3], axis=1)
    total_rows = dp_count * group_rows
    row_top = joint.reshape(total_rows)
    row_total = row_total.reshape(total_rows)
    spread = spread.reshape(total_rows)
    picked = picked.reshape(total_rows)

    log_total = jnp.log(row_total)
    logprob = picked - row_top - log_total
    entropy = log_total - spread / row_total
    short_count = short_lengths.shape[0]
    long_len = total_rows - short_count * SLOT
    row_ids = lax.iota(jnp.int32, total_rows)
    past_long = row_ids - long_len
    sequence = jnp.where(row_ids < long_len, 0, 1 + past_long // SLOT)
    slot_pos = past_long % SLOT
    seq_lengths = jnp.concatenate([jnp.full((1,), long_len, jnp.int32), short_lengths])
    member = sequence[:, None] == lax.iota(jnp.int32, short_count + 1)[None, :]
    row_length = jnp.sum(jnp.where(member, seq_lengths[None, :], 0), axis=1)
    is_live = (row_ids < long_len) | (slot_pos < row_length)
    logprob = jnp.where(is_live, logprob, jnp.float32(0.0))
    entropy = jnp.where(is_live, entropy, jnp.float32(0.0))
    seq_sums = jnp.stack(
        [
            jnp.sum(jnp.where(member, logprob[:, None], jnp.float32(0.0)), axis=0),
            jnp.sum(jnp.where(member, entropy[:, None], jnp.float32(0.0)), axis=0),
        ]
    )
    seq_means = seq_sums / seq_lengths.astype(jnp.float32)[None, :]
    is_owner = owner == dp_pos
    seq_scores = jnp.where(is_owner[None, :], seq_means, jnp.float32(0.0))[None, :, :]
    me = dp_pos * tensor_count + tensor_pos
    mine = (lax.iota(jnp.int32, devices) == me)[:, None]
    own_logprob = jnp.sum(jnp.where(mine, logprob.reshape(devices, own_rows), 0.0), axis=0)
    own_entropy = jnp.sum(jnp.where(mine, entropy.reshape(devices, own_rows), 0.0), axis=0)
    return (own_logprob, own_entropy, seq_scores)


def solution(mesh):
    return jax.shard_map(
        body,
        mesh=mesh,
        in_specs=(P(("dp", "tensor"), None), P(), P(None, "tensor"), P(("dp", "tensor")), P(), P()),
        out_specs=(P(("dp", "tensor")), P(("dp", "tensor")), P("dp", None, None)),
        check_vma=False,
    )
```

```python
import jax
import jax.numpy as jnp
from jax import lax
from jax.experimental import pallas as pl
from jax.experimental.pallas import tpu as pltpu
from jax.sharding import PartitionSpec as P

SLOT = 64
DIGIT = 256
PAD_COLS = 128
LOW_GROUP = 4
CHUNKS = 8


def pack_kernel(tgt_ref, hidden_ref, gain_ref, o_ref):
    rows, features = hidden_ref.shape
    values = hidden_ref[...].astype(jnp.float32)
    scale = lax.rsqrt(jnp.sum(values * values, axis=1, keepdims=True) / features + 1e-06)
    o_ref[:, :features] = (values * scale * gain_ref[...]).astype(jnp.bfloat16)
    place = lax.broadcasted_iota(jnp.int32, (rows, PAD_COLS), 1)
    row = lax.broadcasted_iota(jnp.int32, (rows, PAD_COLS), 0)
    target = jnp.zeros((rows, PAD_COLS), jnp.int32)
    for r in range(rows):
        target = jnp.where(row == r, tgt_ref[r], target)
    digit = jnp.where(place == 1, target // DIGIT, jnp.where(place == 2, target // (DIGIT * DIGIT), target))
    digit = jnp.where(place < 3, digit % DIGIT, 0)
    o_ref[:, features:] = digit.astype(jnp.float32).astype(jnp.bfloat16)


def pack_rows(hidden, gain, targets):
    rows, features = hidden.shape
    return pl.pallas_call(
        pack_kernel,
        in_specs=[
            pl.BlockSpec(memory_space=pltpu.SMEM),
            pl.BlockSpec((rows, features), lambda: (0, 0)),
            pl.BlockSpec((1, features), lambda: (0, 0)),
        ],
        out_specs=pl.BlockSpec((rows, features + PAD_COLS), lambda: (0, 0)),
        out_shape=jax.ShapeDtypeStruct((rows, features + PAD_COLS), jnp.bfloat16),
    )(targets, hidden, gain.reshape(1, features))


def gather_rows(packed, tensor_pos, tensor_count):
    high = tensor_count // LOW_GROUP
    if tensor_count % LOW_GROUP or high & (high - 1) or high == 1:
        return lax.all_gather(packed, "tensor", axis=0, tiled=True), lambda stats: stats
    blocks = [packed] + [
        lax.ppermute(packed, "tensor", [(i, i ^ (k * LOW_GROUP)) for i in range(tensor_count)])
        for k in range(1, high)
    ]
    groups = [[h * LOW_GROUP + low for low in range(LOW_GROUP)] for h in range(high)]
    gathered = lax.all_gather(
        jnp.concatenate(blocks, axis=0), "tensor", axis=0, tiled=True, axis_index_groups=groups
    )
    own_rows = packed.shape[0]
    order = lax.iota(jnp.int32, high) ^ (tensor_pos // LOW_GROUP)

    def restore(stats):
        stats = stats.reshape(stats.shape[0], LOW_GROUP, high, own_rows)
        stats = jnp.take(stats, order, axis=2)
        return stats.transpose(0, 2, 1, 3).reshape(stats.shape[0], tensor_count * own_rows)

    return gathered, restore


def chunk_stats(normed_rows, target_rows, weight, offset):
    logits = jnp.dot(normed_rows, weight, preferred_element_type=jnp.float32)
    row_top = jnp.max(logits, axis=1)
    shifted = logits - row_top[:, None]
    weights_exp = jnp.exp(shifted)
    row_total = jnp.sum(weights_exp, axis=1)
    spread = jnp.sum(weights_exp * shifted, axis=1)
    columns = lax.iota(jnp.int32, weight.shape[1]) + offset
    is_target = target_rows[:, None] == columns[None, :]
    picked = jnp.sum(jnp.where(is_target, logits, jnp.float32(0.0)), axis=1)
    return (row_top, row_total, spread, picked)


def local_stats(normed_rows, target_rows, weight, offset):
    width = weight.shape[1]
    chunks = CHUNKS if width % CHUNKS == 0 else 1
    step = width // chunks
    parts = []
    for c in range(chunks):
        part = chunk_stats(normed_rows, target_rows, weight[:, c * step:(c + 1) * step], offset + c * step)
        part, normed_rows = lax.optimization_barrier((part, normed_rows))
        parts.append(part)
    top = parts[0][0]
    for part in parts[1:]:
        top = jnp.maximum(top, part[0])
    total = jnp.zeros_like(top)
    spread = jnp.zeros_like(top)
    picked = jnp.zeros_like(top)
    for part in parts:
        factor = jnp.exp(part[0] - top)
        total = total + part[1] * factor
        spread = spread + factor * (part[2] + part[1] * (part[0] - top))
        picked = picked + part[3]
    return jnp.stack([top, total, spread, picked])


def body(hidden, gain, head_weight, targets, short_lengths, owner):
    own_rows, features = hidden.shape
    dp_pos = lax.axis_index("dp")
    dp_count = lax.axis_size("dp")
    tensor_pos = lax.axis_index("tensor")
    tensor_count = lax.axis_size("tensor")
    offset = tensor_pos * head_weight.shape[1]
    packed = pack_rows(hidden, gain, targets)
    gathered, restore = gather_rows(packed, tensor_pos, tensor_count)
    rows_normed = gathered[:, :features]
    got = gathered[:, features:features + 3].astype(jnp.int32)
    rows_targets = got[:, 0] + DIGIT * got[:, 1] + (DIGIT * DIGIT) * got[:, 2]

    stats = restore(local_stats(rows_normed, rows_targets, head_weight, offset))
    group_rows = stats.shape[1]
    devices = dp_count * tensor_count
    sent = jnp.broadcast_to(stats[None], (devices,) + stats.shape)
    everything = lax.all_to_all(sent, ("dp", "tensor"), 0, 0, tiled=True)
    everything = everything.reshape(dp_count, tensor_count, 4, group_rows)
    tops = everything[:, :, 0]
    joint = jnp.max(tops, axis=1)
    factor = jnp.exp(tops - joint[:, None, :])
    totals = everything[:, :, 1]
    row_total = jnp.sum(totals * factor, axis=1)
    spread = jnp.sum(factor * (everything[:, :, 2] + totals * (tops - joint[:, None, :])), axis=1)
    picked = jnp.sum(everything[:, :, 3], axis=1)
    total_rows = dp_count * group_rows
    row_top = joint.reshape(total_rows)
    row_total = row_total.reshape(total_rows)
    spread = spread.reshape(total_rows)
    picked = picked.reshape(total_rows)

    log_total = jnp.log(row_total)
    logprob = picked - row_top - log_total
    entropy = log_total - spread / row_total
    short_count = short_lengths.shape[0]
    long_len = total_rows - short_count * SLOT
    row_ids = lax.iota(jnp.int32, total_rows)
    past_long = row_ids - long_len
    sequence = jnp.where(row_ids < long_len, 0, 1 + past_long // SLOT)
    slot_pos = past_long % SLOT
    seq_lengths = jnp.concatenate([jnp.full((1,), long_len, jnp.int32), short_lengths])
    member = sequence[:, None] == lax.iota(jnp.int32, short_count + 1)[None, :]
    row_length = jnp.sum(jnp.where(member, seq_lengths[None, :], 0), axis=1)
    is_live = (row_ids < long_len) | (slot_pos < row_length)
    logprob = jnp.where(is_live, logprob, jnp.float32(0.0))
    entropy = jnp.where(is_live, entropy, jnp.float32(0.0))
    seq_sums = jnp.stack(
        [
            jnp.sum(jnp.where(member, logprob[:, None], jnp.float32(0.0)), axis=0),
            jnp.sum(jnp.where(member, entropy[:, None], jnp.float32(0.0)), axis=0),
        ]
    )
    seq_means = seq_sums / seq_lengths.astype(jnp.float32)[None, :]
    is_owner = owner == dp_pos
    seq_scores = jnp.where(is_owner[None, :], seq_means, jnp.float32(0.0))[None, :, :]
    me = dp_pos * tensor_count + tensor_pos
    mine = (lax.iota(jnp.int32, devices) == me)[:, None]
    own_logprob = jnp.sum(jnp.where(mine, logprob.reshape(devices, own_rows), 0.0), axis=0)
    own_entropy = jnp.sum(jnp.where(mine, entropy.reshape(devices, own_rows), 0.0), axis=0)
    return (own_logprob, own_entropy, seq_scores)


def solution(mesh):
    return jax.shard_map(
        body,
        mesh=mesh,
        in_specs=(P(("dp", "tensor"), None), P(), P(None, "tensor"), P(("dp", "tensor")), P(), P()),
        out_specs=(P(("dp", "tensor")), P(("dp", "tensor")), P("dp", None, None)),
        check_vma=False,
    )
```

```python
import jax
import jax.numpy as jnp
from jax import lax
from jax.experimental import pallas as pl
from jax.experimental.pallas import tpu as pltpu
from jax.sharding import PartitionSpec as P

SLOT = 64
DIGIT = 256
PAD_COLS = 128
LOW_GROUP = 4
CHUNKS = 2


def pack_kernel(tgt_ref, hidden_ref, gain_ref, o_ref):
    rows, features = hidden_ref.shape
    values = hidden_ref[...].astype(jnp.float32)
    scale = lax.rsqrt(jnp.sum(values * values, axis=1, keepdims=True) / features + 1e-06)
    o_ref[:, :features] = (values * scale * gain_ref[...]).astype(jnp.bfloat16)
    place = lax.broadcasted_iota(jnp.int32, (rows, PAD_COLS), 1)
    row = lax.broadcasted_iota(jnp.int32, (rows, PAD_COLS), 0)
    target = jnp.zeros((rows, PAD_COLS), jnp.int32)
    for r in range(rows):
        target = jnp.where(row == r, tgt_ref[r], target)
    digit = jnp.where(place == 1, target // DIGIT, jnp.where(place == 2, target // (DIGIT * DIGIT), target))
    digit = jnp.where(place < 3, digit % DIGIT, 0)
    o_ref[:, features:] = digit.astype(jnp.float32).astype(jnp.bfloat16)


def pack_rows(hidden, gain, targets):
    rows, features = hidden.shape
    return pl.pallas_call(
        pack_kernel,
        in_specs=[
            pl.BlockSpec(memory_space=pltpu.SMEM),
            pl.BlockSpec((rows, features), lambda: (0, 0)),
            pl.BlockSpec((1, features), lambda: (0, 0)),
        ],
        out_specs=pl.BlockSpec((rows, features + PAD_COLS), lambda: (0, 0)),
        out_shape=jax.ShapeDtypeStruct((rows, features + PAD_COLS), jnp.bfloat16),
    )(targets, hidden, gain.reshape(1, features))


def gather_rows(packed, tensor_pos, tensor_count):
    high = tensor_count // LOW_GROUP
    if tensor_count % LOW_GROUP or high & (high - 1) or high == 1:
        return lax.all_gather(packed, "tensor", axis=0, tiled=True), lambda stats: stats
    blocks = [packed] + [
        lax.ppermute(packed, "tensor", [(i, i ^ (k * LOW_GROUP)) for i in range(tensor_count)])
        for k in range(1, high)
    ]
    groups = [[h * LOW_GROUP + low for low in range(LOW_GROUP)] for h in range(high)]
    gathered = lax.all_gather(
        jnp.concatenate(blocks, axis=0), "tensor", axis=0, tiled=True, axis_index_groups=groups
    )
    own_rows = packed.shape[0]
    order = lax.iota(jnp.int32, high) ^ (tensor_pos // LOW_GROUP)

    def restore(stats):
        stats = stats.reshape(stats.shape[0], LOW_GROUP, high, own_rows)
        stats = jnp.take(stats, order, axis=2)
        return stats.transpose(0, 2, 1, 3).reshape(stats.shape[0], tensor_count * own_rows)

    return gathered, restore


def chunk_stats(normed_rows, target_rows, weight, offset):
    logits = jnp.dot(normed_rows, weight, preferred_element_type=jnp.float32)
    row_top = jnp.max(logits, axis=1)
    shifted = logits - row_top[:, None]
    weights_exp = jnp.exp(shifted)
    row_total = jnp.sum(weights_exp, axis=1)
    spread = jnp.sum(weights_exp * shifted, axis=1)
    columns = lax.iota(jnp.int32, weight.shape[1]) + offset
    is_target = target_rows[:, None] == columns[None, :]
    picked = jnp.sum(jnp.where(is_target, logits, jnp.float32(0.0)), axis=1)
    return (row_top, row_total, spread, picked)


def local_stats(normed_rows, target_rows, weight, offset):
    width = weight.shape[1]
    chunks = CHUNKS if width % CHUNKS == 0 else 1
    step = width // chunks
    parts = []
    for c in range(chunks):
        part = chunk_stats(normed_rows, target_rows, weight[:, c * step:(c + 1) * step], offset + c * step)
        part, normed_rows = lax.optimization_barrier((part, normed_rows))
        parts.append(part)
    top = parts[0][0]
    for part in parts[1:]:
        top = jnp.maximum(top, part[0])
    total = jnp.zeros_like(top)
    spread = jnp.zeros_like(top)
    picked = jnp.zeros_like(top)
    for part in parts:
        factor = jnp.exp(part[0] - top)
        total = total + part[1] * factor
        spread = spread + factor * (part[2] + part[1] * (part[0] - top))
        picked = picked + part[3]
    return jnp.stack([top, total, spread, picked])


def body(hidden, gain, head_weight, targets, short_lengths, owner):
    own_rows, features = hidden.shape
    dp_pos = lax.axis_index("dp")
    dp_count = lax.axis_size("dp")
    tensor_pos = lax.axis_index("tensor")
    tensor_count = lax.axis_size("tensor")
    offset = tensor_pos * head_weight.shape[1]
    packed = pack_rows(hidden, gain, targets)
    gathered, restore = gather_rows(packed, tensor_pos, tensor_count)
    rows_normed = gathered[:, :features]
    got = gathered[:, features:features + 3].astype(jnp.int32)
    rows_targets = got[:, 0] + DIGIT * got[:, 1] + (DIGIT * DIGIT) * got[:, 2]

    stats = restore(local_stats(rows_normed, rows_targets, head_weight, offset))
    group_rows = stats.shape[1]
    devices = dp_count * tensor_count
    sent = jnp.broadcast_to(stats[None], (devices,) + stats.shape)
    everything = lax.all_to_all(sent, ("dp", "tensor"), 0, 0, tiled=True)
    everything = everything.reshape(dp_count, tensor_count, 4, group_rows)
    tops = everything[:, :, 0]
    joint = jnp.max(tops, axis=1)
    factor = jnp.exp(tops - joint[:, None, :])
    totals = everything[:, :, 1]
    row_total = jnp.sum(totals * factor, axis=1)
    spread = jnp.sum(factor * (everything[:, :, 2] + totals * (tops - joint[:, None, :])), axis=1)
    picked = jnp.sum(everything[:, :, 3], axis=1)
    total_rows = dp_count * group_rows
    row_top = joint.reshape(total_rows)
    row_total = row_total.reshape(total_rows)
    spread = spread.reshape(total_rows)
    picked = picked.reshape(total_rows)

    log_total = jnp.log(row_total)
    logprob = picked - row_top - log_total
    entropy = log_total - spread / row_total
    short_count = short_lengths.shape[0]
    long_len = total_rows - short_count * SLOT
    row_ids = lax.iota(jnp.int32, total_rows)
    past_long = row_ids - long_len
    sequence = jnp.where(row_ids < long_len, 0, 1 + past_long // SLOT)
    slot_pos = past_long % SLOT
    seq_lengths = jnp.concatenate([jnp.full((1,), long_len, jnp.int32), short_lengths])
    member = sequence[:, None] == lax.iota(jnp.int32, short_count + 1)[None, :]
    row_length = jnp.sum(jnp.where(member, seq_lengths[None, :], 0), axis=1)
    is_live = (row_ids < long_len) | (slot_pos < row_length)
    logprob = jnp.where(is_live, logprob, jnp.float32(0.0))
    entropy = jnp.where(is_live, entropy, jnp.float32(0.0))
    seq_sums = jnp.stack(
        [
            jnp.sum(jnp.where(member, logprob[:, None], jnp.float32(0.0)), axis=0),
            jnp.sum(jnp.where(member, entropy[:, None], jnp.float32(0.0)), axis=0),
        ]
    )
    seq_means = seq_sums / seq_lengths.astype(jnp.float32)[None, :]
    is_owner = owner == dp_pos
    seq_scores = jnp.where(is_owner[None, :], seq_means, jnp.float32(0.0))[None, :, :]
    me = dp_pos * tensor_count + tensor_pos
    mine = (lax.iota(jnp.int32, devices) == me)[:, None]
    own_logprob = jnp.sum(jnp.where(mine, logprob.reshape(devices, own_rows), 0.0), axis=0)
    own_entropy = jnp.sum(jnp.where(mine, entropy.reshape(devices, own_rows), 0.0), axis=0)
    return (own_logprob, own_entropy, seq_scores)


def solution(mesh):
    return jax.shard_map(
        body,
        mesh=mesh,
        in_specs=(P(("dp", "tensor"), None), P(), P(None, "tensor"), P(("dp", "tensor")), P(), P()),
        out_specs=(P(("dp", "tensor")), P(("dp", "tensor")), P("dp", None, None)),
        check_vma=False,
    )
```

```python
import jax
import jax.numpy as jnp
from jax import lax
from jax.experimental import pallas as pl
from jax.experimental.pallas import tpu as pltpu
from jax.sharding import PartitionSpec as P

SLOT = 64
DIGIT = 256
PAD_COLS = 128
LOW_GROUP = 4
CHUNKS = 4


def pack_kernel(tgt_ref, hidden_ref, gain_ref, o_ref):
    rows, features = hidden_ref.shape
    values = hidden_ref[...].astype(jnp.float32)
    scale = lax.rsqrt(jnp.sum(values * values, axis=1, keepdims=True) / features + 1e-06)
    o_ref[:, :features] = (values * scale * gain_ref[...]).astype(jnp.bfloat16)
    place = lax.broadcasted_iota(jnp.int32, (rows, PAD_COLS), 1)
    row = lax.broadcasted_iota(jnp.int32, (rows, PAD_COLS), 0)
    target = jnp.zeros((rows, PAD_COLS), jnp.int32)
    for r in range(rows):
        target = jnp.where(row == r, tgt_ref[r], target)
    digit = jnp.where(place == 1, target // DIGIT, jnp.where(place == 2, target // (DIGIT * DIGIT), target))
    digit = jnp.where(place < 3, digit % DIGIT, 0)
    o_ref[:, features:] = digit.astype(jnp.float32).astype(jnp.bfloat16)


def pack_rows(hidden, gain, targets):
    rows, features = hidden.shape
    return pl.pallas_call(
        pack_kernel,
        in_specs=[
            pl.BlockSpec(memory_space=pltpu.SMEM),
            pl.BlockSpec((rows, features), lambda: (0, 0)),
            pl.BlockSpec((1, features), lambda: (0, 0)),
        ],
        out_specs=pl.BlockSpec((rows, features + PAD_COLS), lambda: (0, 0)),
        out_shape=jax.ShapeDtypeStruct((rows, features + PAD_COLS), jnp.bfloat16),
    )(targets, hidden, gain.reshape(1, features))


def gather_rows(packed, tensor_pos, tensor_count):
    high = tensor_count // LOW_GROUP
    if tensor_count % LOW_GROUP or high & (high - 1) or high == 1:
        return lax.all_gather(packed, "tensor", axis=0, tiled=True), lambda stats: stats
    blocks = [packed] + [
        lax.ppermute(packed, "tensor", [(i, i ^ (k * LOW_GROUP)) for i in range(tensor_count)])
        for k in range(1, high)
    ]
    groups = [[h * LOW_GROUP + low for low in range(LOW_GROUP)] for h in range(high)]
    gathered = lax.all_gather(
        jnp.concatenate(blocks, axis=0), "tensor", axis=0, tiled=True, axis_index_groups=groups
    )
    own_rows = packed.shape[0]
    order = lax.iota(jnp.int32, high) ^ (tensor_pos // LOW_GROUP)

    def restore(stats):
        stats = stats.reshape(stats.shape[0], LOW_GROUP, high, own_rows)
        stats = jnp.take(stats, order, axis=2)
        return stats.transpose(0, 2, 1, 3).reshape(stats.shape[0], tensor_count * own_rows)

    return gathered, restore


def chunk_stats(normed_rows, target_rows, weight, offset):
    logits = jnp.dot(normed_rows, weight, preferred_element_type=jnp.float32)
    row_top = jnp.max(logits, axis=1)
    shifted = logits - row_top[:, None]
    weights_exp = jnp.exp(shifted)
    row_total = jnp.sum(weights_exp, axis=1)
    spread = jnp.sum(weights_exp * shifted, axis=1)
    columns = lax.iota(jnp.int32, weight.shape[1]) + offset
    is_target = target_rows[:, None] == columns[None, :]
    picked = jnp.sum(jnp.where(is_target, logits, jnp.float32(0.0)), axis=1)
    return (row_top, row_total, spread, picked)


def local_stats(normed_rows, target_rows, weight, offset):
    width = weight.shape[1]
    step = (width // CHUNKS) // 128 * 128
    chunks = CHUNKS if step else 1
    edges = [c * step for c in range(chunks)] + [width]
    parts = []
    for c in range(chunks):
        begin, end = edges[c], edges[c + 1]
        part = chunk_stats(normed_rows, target_rows, weight[:, begin:end], offset + begin)
        part, normed_rows = lax.optimization_barrier((part, normed_rows))
        parts.append(part)
    top = parts[0][0]
    for part in parts[1:]:
        top = jnp.maximum(top, part[0])
    total = jnp.zeros_like(top)
    spread = jnp.zeros_like(top)
    picked = jnp.zeros_like(top)
    for part in parts:
        factor = jnp.exp(part[0] - top)
        total = total + part[1] * factor
        spread = spread + factor * (part[2] + part[1] * (part[0] - top))
        picked = picked + part[3]
    return jnp.stack([top, total, spread, picked])


def body(hidden, gain, head_weight, targets, short_lengths, owner):
    own_rows, features = hidden.shape
    dp_pos = lax.axis_index("dp")
    dp_count = lax.axis_size("dp")
    tensor_pos = lax.axis_index("tensor")
    tensor_count = lax.axis_size("tensor")
    offset = tensor_pos * head_weight.shape[1]
    packed = pack_rows(hidden, gain, targets)
    gathered, restore = gather_rows(packed, tensor_pos, tensor_count)
    rows_normed = gathered[:, :features]
    got = gathered[:, features:features + 3].astype(jnp.int32)
    rows_targets = got[:, 0] + DIGIT * got[:, 1] + (DIGIT * DIGIT) * got[:, 2]

    stats = restore(local_stats(rows_normed, rows_targets, head_weight, offset))
    group_rows = stats.shape[1]
    devices = dp_count * tensor_count
    sent = jnp.broadcast_to(stats[None], (devices,) + stats.shape)
    everything = lax.all_to_all(sent, ("dp", "tensor"), 0, 0, tiled=True)
    everything = everything.reshape(dp_count, tensor_count, 4, group_rows)
    tops = everything[:, :, 0]
    joint = jnp.max(tops, axis=1)
    factor = jnp.exp(tops - joint[:, None, :])
    totals = everything[:, :, 1]
    row_total = jnp.sum(totals * factor, axis=1)
    spread = jnp.sum(factor * (everything[:, :, 2] + totals * (tops - joint[:, None, :])), axis=1)
    picked = jnp.sum(everything[:, :, 3], axis=1)
    total_rows = dp_count * group_rows
    row_top = joint.reshape(total_rows)
    row_total = row_total.reshape(total_rows)
    spread = spread.reshape(total_rows)
    picked = picked.reshape(total_rows)

    log_total = jnp.log(row_total)
    logprob = picked - row_top - log_total
    entropy = log_total - spread / row_total
    short_count = short_lengths.shape[0]
    long_len = total_rows - short_count * SLOT
    row_ids = lax.iota(jnp.int32, total_rows)
    past_long = row_ids - long_len
    sequence = jnp.where(row_ids < long_len, 0, 1 + past_long // SLOT)
    slot_pos = past_long % SLOT
    seq_lengths = jnp.concatenate([jnp.full((1,), long_len, jnp.int32), short_lengths])
    member = sequence[:, None] == lax.iota(jnp.int32, short_count + 1)[None, :]
    row_length = jnp.sum(jnp.where(member, seq_lengths[None, :], 0), axis=1)
    is_live = (row_ids < long_len) | (slot_pos < row_length)
    logprob = jnp.where(is_live, logprob, jnp.float32(0.0))
    entropy = jnp.where(is_live, entropy, jnp.float32(0.0))
    seq_sums = jnp.stack(
        [
            jnp.sum(jnp.where(member, logprob[:, None], jnp.float32(0.0)), axis=0),
            jnp.sum(jnp.where(member, entropy[:, None], jnp.float32(0.0)), axis=0),
        ]
    )
    seq_means = seq_sums / seq_lengths.astype(jnp.float32)[None, :]
    is_owner = owner == dp_pos
    seq_scores = jnp.where(is_owner[None, :], seq_means, jnp.float32(0.0))[None, :, :]
    me = dp_pos * tensor_count + tensor_pos
    mine = (lax.iota(jnp.int32, devices) == me)[:, None]
    own_logprob = jnp.sum(jnp.where(mine, logprob.reshape(devices, own_rows), 0.0), axis=0)
    own_entropy = jnp.sum(jnp.where(mine, entropy.reshape(devices, own_rows), 0.0), axis=0)
    return (own_logprob, own_entropy, seq_scores)


def solution(mesh):
    return jax.shard_map(
        body,
        mesh=mesh,
        in_specs=(P(("dp", "tensor"), None), P(), P(None, "tensor"), P(("dp", "tensor")), P(), P()),
        out_specs=(P(("dp", "tensor")), P(("dp", "tensor")), P("dp", None, None)),
        check_vma=False,
    )
```

```python
import jax
import jax.numpy as jnp
from jax import lax
from jax.experimental import pallas as pl
from jax.experimental.pallas import tpu as pltpu
from jax.sharding import PartitionSpec as P

SLOT = 64
DIGIT = 256
PAD_COLS = 128
LOW_GROUP = 4
CHUNKS = 4


def pack_kernel(tgt_ref, hidden_ref, gain_ref, o_ref):
    rows, features = hidden_ref.shape
    values = hidden_ref[...].astype(jnp.float32)
    scale = lax.rsqrt(jnp.sum(values * values, axis=1, keepdims=True) / features + 1e-06)
    o_ref[:, :features] = (values * scale * gain_ref[...]).astype(jnp.bfloat16)
    place = lax.broadcasted_iota(jnp.int32, (rows, PAD_COLS), 1)
    row = lax.broadcasted_iota(jnp.int32, (rows, PAD_COLS), 0)
    target = jnp.zeros((rows, PAD_COLS), jnp.int32)
    for r in range(rows):
        target = jnp.where(row == r, tgt_ref[r], target)
    digit = jnp.where(place == 1, target // DIGIT, jnp.where(place == 2, target // (DIGIT * DIGIT), target))
    digit = jnp.where(place < 3, digit % DIGIT, 0)
    o_ref[:, features:] = digit.astype(jnp.float32).astype(jnp.bfloat16)


def pack_rows(hidden, gain, targets):
    rows, features = hidden.shape
    return pl.pallas_call(
        pack_kernel,
        in_specs=[
            pl.BlockSpec(memory_space=pltpu.SMEM),
            pl.BlockSpec((rows, features), lambda: (0, 0)),
            pl.BlockSpec((1, features), lambda: (0, 0)),
        ],
        out_specs=pl.BlockSpec((rows, features + PAD_COLS), lambda: (0, 0)),
        out_shape=jax.ShapeDtypeStruct((rows, features + PAD_COLS), jnp.bfloat16),
    )(targets, hidden, gain.reshape(1, features))


def gather_rows(packed, tensor_pos, tensor_count):
    high = tensor_count // LOW_GROUP
    if tensor_count % LOW_GROUP or high & (high - 1) or high == 1:
        return lax.all_gather(packed, "tensor", axis=0, tiled=True), lambda stats: stats
    received = [packed] + [
        lax.ppermute(packed, "tensor", [(i, i ^ (k * LOW_GROUP)) for i in range(tensor_count)])
        for k in range(1, high)
    ]
    own_high = tensor_pos // LOW_GROUP
    blocks = []
    for h in range(high):
        block = received[0]
        for k in range(1, high):
            block = jnp.where((own_high ^ h) == k, received[k], block)
        blocks.append(block)
    groups = [[h * LOW_GROUP + low for low in range(LOW_GROUP)] for h in range(high)]
    gathered = lax.all_gather(
        jnp.concatenate(blocks, axis=0), "tensor", axis=0, tiled=True, axis_index_groups=groups
    )
    own_rows = packed.shape[0]

    def restore(stats):
        stats = stats.reshape(stats.shape[0], LOW_GROUP, high, own_rows)
        return stats.transpose(0, 2, 1, 3).reshape(stats.shape[0], tensor_count * own_rows)

    return gathered, restore


def chunk_stats(normed_rows, target_rows, weight, offset):
    logits = jnp.dot(normed_rows, weight, preferred_element_type=jnp.float32)
    row_top = jnp.max(logits, axis=1)
    shifted = logits - row_top[:, None]
    weights_exp = jnp.exp(shifted)
    row_total = jnp.sum(weights_exp, axis=1)
    spread = jnp.sum(weights_exp * shifted, axis=1)
    columns = lax.iota(jnp.int32, weight.shape[1]) + offset
    is_target = target_rows[:, None] == columns[None, :]
    picked = jnp.sum(jnp.where(is_target, logits, jnp.float32(0.0)), axis=1)
    return (row_top, row_total, spread, picked)


def local_stats(normed_rows, target_rows, weight, offset):
    width = weight.shape[1]
    chunks = CHUNKS if width % CHUNKS == 0 else 1
    step = width // chunks
    parts = []
    for c in range(chunks):
        part = chunk_stats(normed_rows, target_rows, weight[:, c * step:(c + 1) * step], offset + c * step)
        part, normed_rows = lax.optimization_barrier((part, normed_rows))
        parts.append(part)
    top = parts[0][0]
    for part in parts[1:]:
        top = jnp.maximum(top, part[0])
    total = jnp.zeros_like(top)
    spread = jnp.zeros_like(top)
    picked = jnp.zeros_like(top)
    for part in parts:
        factor = jnp.exp(part[0] - top)
        total = total + part[1] * factor
        spread = spread + factor * (part[2] + part[1] * (part[0] - top))
        picked = picked + part[3]
    return jnp.stack([top, total, spread, picked])


def body(hidden, gain, head_weight, targets, short_lengths, owner):
    own_rows, features = hidden.shape
    dp_pos = lax.axis_index("dp")
    dp_count = lax.axis_size("dp")
    tensor_pos = lax.axis_index("tensor")
    tensor_count = lax.axis_size("tensor")
    offset = tensor_pos * head_weight.shape[1]
    packed = pack_rows(hidden, gain, targets)
    gathered, restore = gather_rows(packed, tensor_pos, tensor_count)
    rows_normed = gathered[:, :features]
    got = gathered[:, features:features + 3].astype(jnp.int32)
    rows_targets = got[:, 0] + DIGIT * got[:, 1] + (DIGIT * DIGIT) * got[:, 2]

    stats = restore(local_stats(rows_normed, rows_targets, head_weight, offset))
    group_rows = stats.shape[1]
    devices = dp_count * tensor_count
    sent = jnp.broadcast_to(stats[None], (devices,) + stats.shape)
    everything = lax.all_to_all(sent, ("dp", "tensor"), 0, 0, tiled=True)
    everything = everything.reshape(dp_count, tensor_count, 4, group_rows)
    tops = everything[:, :, 0]
    joint = jnp.max(tops, axis=1)
    factor = jnp.exp(tops - joint[:, None, :])
    totals = everything[:, :, 1]
    row_total = jnp.sum(totals * factor, axis=1)
    spread = jnp.sum(factor * (everything[:, :, 2] + totals * (tops - joint[:, None, :])), axis=1)
    picked = jnp.sum(everything[:, :, 3], axis=1)
    total_rows = dp_count * group_rows
    row_top = joint.reshape(total_rows)
    row_total = row_total.reshape(total_rows)
    spread = spread.reshape(total_rows)
    picked = picked.reshape(total_rows)

    log_total = jnp.log(row_total)
    logprob = picked - row_top - log_total
    entropy = log_total - spread / row_total
    short_count = short_lengths.shape[0]
    long_len = total_rows - short_count * SLOT
    row_ids = lax.iota(jnp.int32, total_rows)
    past_long = row_ids - long_len
    sequence = jnp.where(row_ids < long_len, 0, 1 + past_long // SLOT)
    slot_pos = past_long % SLOT
    seq_lengths = jnp.concatenate([jnp.full((1,), long_len, jnp.int32), short_lengths])
    member = sequence[:, None] == lax.iota(jnp.int32, short_count + 1)[None, :]
    row_length = jnp.sum(jnp.where(member, seq_lengths[None, :], 0), axis=1)
    is_live = (row_ids < long_len) | (slot_pos < row_length)
    logprob = jnp.where(is_live, logprob, jnp.float32(0.0))
    entropy = jnp.where(is_live, entropy, jnp.float32(0.0))
    seq_sums = jnp.stack(
        [
            jnp.sum(jnp.where(member, logprob[:, None], jnp.float32(0.0)), axis=0),
            jnp.sum(jnp.where(member, entropy[:, None], jnp.float32(0.0)), axis=0),
        ]
    )
    seq_means = seq_sums / seq_lengths.astype(jnp.float32)[None, :]
    is_owner = owner == dp_pos
    seq_scores = jnp.where(is_owner[None, :], seq_means, jnp.float32(0.0))[None, :, :]
    me = dp_pos * tensor_count + tensor_pos
    mine = (lax.iota(jnp.int32, devices) == me)[:, None]
    own_logprob = jnp.sum(jnp.where(mine, logprob.reshape(devices, own_rows), 0.0), axis=0)
    own_entropy = jnp.sum(jnp.where(mine, entropy.reshape(devices, own_rows), 0.0), axis=0)
    return (own_logprob, own_entropy, seq_scores)


def solution(mesh):
    return jax.shard_map(
        body,
        mesh=mesh,
        in_specs=(P(("dp", "tensor"), None), P(), P(None, "tensor"), P(("dp", "tensor")), P(), P()),
        out_specs=(P(("dp", "tensor")), P(("dp", "tensor")), P("dp", None, None)),
        check_vma=False,
    )
```

```python
import jax
import jax.numpy as jnp
from jax import lax
from jax.experimental import pallas as pl
from jax.experimental.pallas import tpu as pltpu
from jax.sharding import PartitionSpec as P

SLOT = 64
DIGIT = 256
PAD_COLS = 128
LOW_GROUP = 4
CHUNK_EDGES = (0.125, 0.375, 0.625)


def pack_kernel(tgt_ref, hidden_ref, gain_ref, o_ref):
    rows, features = hidden_ref.shape
    values = hidden_ref[...].astype(jnp.float32)
    scale = lax.rsqrt(jnp.sum(values * values, axis=1, keepdims=True) / features + 1e-06)
    o_ref[:, :features] = (values * scale * gain_ref[...]).astype(jnp.bfloat16)
    place = lax.broadcasted_iota(jnp.int32, (rows, PAD_COLS), 1)
    row = lax.broadcasted_iota(jnp.int32, (rows, PAD_COLS), 0)
    target = jnp.zeros((rows, PAD_COLS), jnp.int32)
    for r in range(rows):
        target = jnp.where(row == r, tgt_ref[r], target)
    digit = jnp.where(place == 1, target // DIGIT, jnp.where(place == 2, target // (DIGIT * DIGIT), target))
    digit = jnp.where(place < 3, digit % DIGIT, 0)
    o_ref[:, features:] = digit.astype(jnp.float32).astype(jnp.bfloat16)


def pack_rows(hidden, gain, targets):
    rows, features = hidden.shape
    return pl.pallas_call(
        pack_kernel,
        in_specs=[
            pl.BlockSpec(memory_space=pltpu.SMEM),
            pl.BlockSpec((rows, features), lambda: (0, 0)),
            pl.BlockSpec((1, features), lambda: (0, 0)),
        ],
        out_specs=pl.BlockSpec((rows, features + PAD_COLS), lambda: (0, 0)),
        out_shape=jax.ShapeDtypeStruct((rows, features + PAD_COLS), jnp.bfloat16),
    )(targets, hidden, gain.reshape(1, features))


def gather_rows(packed, tensor_pos, tensor_count):
    high = tensor_count // LOW_GROUP
    if tensor_count % LOW_GROUP or high & (high - 1) or high == 1:
        return lax.all_gather(packed, "tensor", axis=0, tiled=True), lambda stats: stats
    received = [packed] + [
        lax.ppermute(packed, "tensor", [(i, i ^ (k * LOW_GROUP)) for i in range(tensor_count)])
        for k in range(1, high)
    ]
    own_high = tensor_pos // LOW_GROUP
    blocks = []
    for h in range(high):
        block = received[0]
        for k in range(1, high):
            block = jnp.where((own_high ^ h) == k, received[k], block)
        blocks.append(block)
    groups = [[h * LOW_GROUP + low for low in range(LOW_GROUP)] for h in range(high)]
    gathered = lax.all_gather(
        jnp.concatenate(blocks, axis=0), "tensor", axis=0, tiled=True, axis_index_groups=groups
    )
    own_rows = packed.shape[0]

    def restore(stats):
        stats = stats.reshape(stats.shape[0], LOW_GROUP, high, own_rows)
        return stats.transpose(0, 2, 1, 3).reshape(stats.shape[0], tensor_count * own_rows)

    return gathered, restore


def chunk_stats(normed_rows, target_rows, weight, offset):
    logits = jnp.dot(normed_rows, weight, preferred_element_type=jnp.float32)
    row_top = jnp.max(logits, axis=1)
    shifted = logits - row_top[:, None]
    weights_exp = jnp.exp(shifted)
    row_total = jnp.sum(weights_exp, axis=1)
    spread = jnp.sum(weights_exp * shifted, axis=1)
    columns = lax.iota(jnp.int32, weight.shape[1]) + offset
    is_target = target_rows[:, None] == columns[None, :]
    picked = jnp.sum(jnp.where(is_target, logits, jnp.float32(0.0)), axis=1)
    return (row_top, row_total, spread, picked)


def local_stats(normed_rows, target_rows, weight, offset):
    width = weight.shape[1]
    edges = [0] + [int(width * share) // 128 * 128 for share in CHUNK_EDGES] + [width]
    if any(b <= a for a, b in zip(edges, edges[1:])):
        edges = [0, width]
    parts = []
    for begin, end in zip(edges, edges[1:]):
        part = chunk_stats(normed_rows, target_rows, weight[:, begin:end], offset + begin)
        part, normed_rows = lax.optimization_barrier((part, normed_rows))
        parts.append(part)
    top = parts[0][0]
    for part in parts[1:]:
        top = jnp.maximum(top, part[0])
    total = jnp.zeros_like(top)
    spread = jnp.zeros_like(top)
    picked = jnp.zeros_like(top)
    for part in parts:
        factor = jnp.exp(part[0] - top)
        total = total + part[1] * factor
        spread = spread + factor * (part[2] + part[1] * (part[0] - top))
        picked = picked + part[3]
    return jnp.stack([top, total, spread, picked])


def body(hidden, gain, head_weight, targets, short_lengths, owner):
    own_rows, features = hidden.shape
    dp_pos = lax.axis_index("dp")
    dp_count = lax.axis_size("dp")
    tensor_pos = lax.axis_index("tensor")
    tensor_count = lax.axis_size("tensor")
    offset = tensor_pos * head_weight.shape[1]
    packed = pack_rows(hidden, gain, targets)
    gathered, restore = gather_rows(packed, tensor_pos, tensor_count)
    rows_normed = gathered[:, :features]
    got = gathered[:, features:features + 3].astype(jnp.int32)
    rows_targets = got[:, 0] + DIGIT * got[:, 1] + (DIGIT * DIGIT) * got[:, 2]

    stats = restore(local_stats(rows_normed, rows_targets, head_weight, offset))
    group_rows = stats.shape[1]
    devices = dp_count * tensor_count
    sent = jnp.broadcast_to(stats[None], (devices,) + stats.shape)
    everything = lax.all_to_all(sent, ("dp", "tensor"), 0, 0, tiled=True)
    everything = everything.reshape(dp_count, tensor_count, 4, group_rows)
    tops = everything[:, :, 0]
    joint = jnp.max(tops, axis=1)
    factor = jnp.exp(tops - joint[:, None, :])
    totals = everything[:, :, 1]
    row_total = jnp.sum(totals * factor, axis=1)
    spread = jnp.sum(factor * (everything[:, :, 2] + totals * (tops - joint[:, None, :])), axis=1)
    picked = jnp.sum(everything[:, :, 3], axis=1)
    total_rows = dp_count * group_rows
    row_top = joint.reshape(total_rows)
    row_total = row_total.reshape(total_rows)
    spread = spread.reshape(total_rows)
    picked = picked.reshape(total_rows)

    log_total = jnp.log(row_total)
    logprob = picked - row_top - log_total
    entropy = log_total - spread / row_total
    short_count = short_lengths.shape[0]
    long_len = total_rows - short_count * SLOT
    row_ids = lax.iota(jnp.int32, total_rows)
    past_long = row_ids - long_len
    sequence = jnp.where(row_ids < long_len, 0, 1 + past_long // SLOT)
    slot_pos = past_long % SLOT
    seq_lengths = jnp.concatenate([jnp.full((1,), long_len, jnp.int32), short_lengths])
    member = sequence[:, None] == lax.iota(jnp.int32, short_count + 1)[None, :]
    row_length = jnp.sum(jnp.where(member, seq_lengths[None, :], 0), axis=1)
    is_live = (row_ids < long_len) | (slot_pos < row_length)
    logprob = jnp.where(is_live, logprob, jnp.float32(0.0))
    entropy = jnp.where(is_live, entropy, jnp.float32(0.0))
    seq_sums = jnp.stack(
        [
            jnp.sum(jnp.where(member, logprob[:, None], jnp.float32(0.0)), axis=0),
            jnp.sum(jnp.where(member, entropy[:, None], jnp.float32(0.0)), axis=0),
        ]
    )
    seq_means = seq_sums / seq_lengths.astype(jnp.float32)[None, :]
    is_owner = owner == dp_pos
    seq_scores = jnp.where(is_owner[None, :], seq_means, jnp.float32(0.0))[None, :, :]
    me = dp_pos * tensor_count + tensor_pos
    mine = (lax.iota(jnp.int32, devices) == me)[:, None]
    own_logprob = jnp.sum(jnp.where(mine, logprob.reshape(devices, own_rows), 0.0), axis=0)
    own_entropy = jnp.sum(jnp.where(mine, entropy.reshape(devices, own_rows), 0.0), axis=0)
    return (own_logprob, own_entropy, seq_scores)


def solution(mesh):
    return jax.shard_map(
        body,
        mesh=mesh,
        in_specs=(P(("dp", "tensor"), None), P(), P(None, "tensor"), P(("dp", "tensor")), P(), P()),
        out_specs=(P(("dp", "tensor")), P(("dp", "tensor")), P("dp", None, None)),
        check_vma=False,
    )
```

```python
import jax
import jax.numpy as jnp
from jax import lax
from jax.experimental import pallas as pl
from jax.experimental.pallas import tpu as pltpu
from jax.sharding import PartitionSpec as P

SLOT = 64
DIGIT = 256
PAD_COLS = 128
LOW_GROUP = 4
CHUNK_EDGES = (0.125, 0.375, 0.625)


def pack_kernel(tgt_ref, hidden_ref, gain_ref, o_ref):
    rows, features = hidden_ref.shape
    values = hidden_ref[...].astype(jnp.float32)
    scale = lax.rsqrt(jnp.sum(values * values, axis=1, keepdims=True) / features + 1e-06)
    o_ref[:, :features] = (values * scale * gain_ref[...]).astype(jnp.bfloat16)
    place = lax.broadcasted_iota(jnp.int32, (rows, PAD_COLS), 1)
    row = lax.broadcasted_iota(jnp.int32, (rows, PAD_COLS), 0)
    target = jnp.zeros((rows, PAD_COLS), jnp.int32)
    for r in range(rows):
        target = jnp.where(row == r, tgt_ref[r], target)
    digit = jnp.where(place == 1, target // DIGIT, jnp.where(place == 2, target // (DIGIT * DIGIT), target))
    digit = jnp.where(place < 3, digit % DIGIT, 0)
    o_ref[:, features:] = digit.astype(jnp.float32).astype(jnp.bfloat16)


def pack_rows(hidden, gain, targets):
    rows, features = hidden.shape
    return pl.pallas_call(
        pack_kernel,
        in_specs=[
            pl.BlockSpec(memory_space=pltpu.SMEM),
            pl.BlockSpec((rows, features), lambda: (0, 0)),
            pl.BlockSpec((1, features), lambda: (0, 0)),
        ],
        out_specs=pl.BlockSpec((rows, features + PAD_COLS), lambda: (0, 0)),
        out_shape=jax.ShapeDtypeStruct((rows, features + PAD_COLS), jnp.bfloat16),
    )(targets, hidden, gain.reshape(1, features))


def gather_rows(packed, tensor_pos, tensor_count):
    high = tensor_count // LOW_GROUP
    if tensor_count % LOW_GROUP or high & (high - 1) or high == 1:
        return lax.all_gather(packed, "tensor", axis=0, tiled=True), lambda stats: stats
    groups = [[h * LOW_GROUP + low for low in range(LOW_GROUP)] for h in range(high)]
    local = lax.all_gather(packed, "tensor", axis=0, tiled=True, axis_index_groups=groups)
    received = [local] + [
        lax.ppermute(local, "tensor", [(i, i ^ (k * LOW_GROUP)) for i in range(tensor_count)])
        for k in range(1, high)
    ]
    own_high = tensor_pos // LOW_GROUP
    blocks = []
    for h in range(high):
        block = received[0]
        for k in range(1, high):
            block = jnp.where((own_high ^ h) == k, received[k], block)
        blocks.append(block)
    return jnp.concatenate(blocks, axis=0), lambda stats: stats


def chunk_stats(normed_rows, target_rows, weight, offset):
    logits = jnp.dot(normed_rows, weight, preferred_element_type=jnp.float32)
    row_top = jnp.max(logits, axis=1)
    shifted = logits - row_top[:, None]
    weights_exp = jnp.exp(shifted)
    row_total = jnp.sum(weights_exp, axis=1)
    spread = jnp.sum(weights_exp * shifted, axis=1)
    columns = lax.iota(jnp.int32, weight.shape[1]) + offset
    is_target = target_rows[:, None] == columns[None, :]
    picked = jnp.sum(jnp.where(is_target, logits, jnp.float32(0.0)), axis=1)
    return (row_top, row_total, spread, picked)


def local_stats(normed_rows, target_rows, weight, offset):
    width = weight.shape[1]
    edges = [0] + [int(width * share) // 128 * 128 for share in CHUNK_EDGES] + [width]
    if any(b <= a for a, b in zip(edges, edges[1:])):
        edges = [0, width]
    parts = []
    for begin, end in zip(edges, edges[1:]):
        part = chunk_stats(normed_rows, target_rows, weight[:, begin:end], offset + begin)
        part, normed_rows = lax.optimization_barrier((part, normed_rows))
        parts.append(part)
    top = parts[0][0]
    for part in parts[1:]:
        top = jnp.maximum(top, part[0])
    total = jnp.zeros_like(top)
    spread = jnp.zeros_like(top)
    picked = jnp.zeros_like(top)
    for part in parts:
        factor = jnp.exp(part[0] - top)
        total = total + part[1] * factor
        spread = spread + factor * (part[2] + part[1] * (part[0] - top))
        picked = picked + part[3]
    return jnp.stack([top, total, spread, picked])


def body(hidden, gain, head_weight, targets, short_lengths, owner):
    own_rows, features = hidden.shape
    dp_pos = lax.axis_index("dp")
    dp_count = lax.axis_size("dp")
    tensor_pos = lax.axis_index("tensor")
    tensor_count = lax.axis_size("tensor")
    offset = tensor_pos * head_weight.shape[1]
    packed = pack_rows(hidden, gain, targets)
    gathered, restore = gather_rows(packed, tensor_pos, tensor_count)
    rows_normed = gathered[:, :features]
    got = gathered[:, features:features + 3].astype(jnp.int32)
    rows_targets = got[:, 0] + DIGIT * got[:, 1] + (DIGIT * DIGIT) * got[:, 2]

    stats = restore(local_stats(rows_normed, rows_targets, head_weight, offset))
    group_rows = stats.shape[1]
    devices = dp_count * tensor_count
    sent = jnp.broadcast_to(stats[None], (devices,) + stats.shape)
    everything = lax.all_to_all(sent, ("dp", "tensor"), 0, 0, tiled=True)
    everything = everything.reshape(dp_count, tensor_count, 4, group_rows)
    tops = everything[:, :, 0]
    joint = jnp.max(tops, axis=1)
    factor = jnp.exp(tops - joint[:, None, :])
    totals = everything[:, :, 1]
    row_total = jnp.sum(totals * factor, axis=1)
    spread = jnp.sum(factor * (everything[:, :, 2] + totals * (tops - joint[:, None, :])), axis=1)
    picked = jnp.sum(everything[:, :, 3], axis=1)
    total_rows = dp_count * group_rows
    row_top = joint.reshape(total_rows)
    row_total = row_total.reshape(total_rows)
    spread = spread.reshape(total_rows)
    picked = picked.reshape(total_rows)

    log_total = jnp.log(row_total)
    logprob = picked - row_top - log_total
    entropy = log_total - spread / row_total
    short_count = short_lengths.shape[0]
    long_len = total_rows - short_count * SLOT
    row_ids = lax.iota(jnp.int32, total_rows)
    past_long = row_ids - long_len
    sequence = jnp.where(row_ids < long_len, 0, 1 + past_long // SLOT)
    slot_pos = past_long % SLOT
    seq_lengths = jnp.concatenate([jnp.full((1,), long_len, jnp.int32), short_lengths])
    member = sequence[:, None] == lax.iota(jnp.int32, short_count + 1)[None, :]
    row_length = jnp.sum(jnp.where(member, seq_lengths[None, :], 0), axis=1)
    is_live = (row_ids < long_len) | (slot_pos < row_length)
    logprob = jnp.where(is_live, logprob, jnp.float32(0.0))
    entropy = jnp.where(is_live, entropy, jnp.float32(0.0))
    seq_sums = jnp.stack(
        [
            jnp.sum(jnp.where(member, logprob[:, None], jnp.float32(0.0)), axis=0),
            jnp.sum(jnp.where(member, entropy[:, None], jnp.float32(0.0)), axis=0),
        ]
    )
    seq_means = seq_sums / seq_lengths.astype(jnp.float32)[None, :]
    is_owner = owner == dp_pos
    seq_scores = jnp.where(is_owner[None, :], seq_means, jnp.float32(0.0))[None, :, :]
    me = dp_pos * tensor_count + tensor_pos
    mine = (lax.iota(jnp.int32, devices) == me)[:, None]
    own_logprob = jnp.sum(jnp.where(mine, logprob.reshape(devices, own_rows), 0.0), axis=0)
    own_entropy = jnp.sum(jnp.where(mine, entropy.reshape(devices, own_rows), 0.0), axis=0)
    return (own_logprob, own_entropy, seq_scores)


def solution(mesh):
    return jax.shard_map(
        body,
        mesh=mesh,
        in_specs=(P(("dp", "tensor"), None), P(), P(None, "tensor"), P(("dp", "tensor")), P(), P()),
        out_specs=(P(("dp", "tensor")), P(("dp", "tensor")), P("dp", None, None)),
        check_vma=False,
    )
```

```python
import jax
import jax.numpy as jnp
from jax import lax
from jax.experimental import pallas as pl
from jax.experimental.pallas import tpu as pltpu
from jax.sharding import PartitionSpec as P

SLOT = 64
DIGIT = 256
PAD_COLS = 128
LOW_GROUP = 4
CHUNK_EDGES = (0.125, 0.375, 0.75)


def pack_kernel(tgt_ref, hidden_ref, gain_ref, o_ref):
    rows, features = hidden_ref.shape
    values = hidden_ref[...].astype(jnp.float32)
    scale = lax.rsqrt(jnp.sum(values * values, axis=1, keepdims=True) / features + 1e-06)
    o_ref[:, :features] = (values * scale * gain_ref[...]).astype(jnp.bfloat16)
    place = lax.broadcasted_iota(jnp.int32, (rows, PAD_COLS), 1)
    row = lax.broadcasted_iota(jnp.int32, (rows, PAD_COLS), 0)
    target = jnp.zeros((rows, PAD_COLS), jnp.int32)
    for r in range(rows):
        target = jnp.where(row == r, tgt_ref[r], target)
    digit = jnp.where(place == 1, target // DIGIT, jnp.where(place == 2, target // (DIGIT * DIGIT), target))
    digit = jnp.where(place < 3, digit % DIGIT, 0)
    o_ref[:, features:] = digit.astype(jnp.float32).astype(jnp.bfloat16)


def pack_rows(hidden, gain, targets):
    rows, features = hidden.shape
    return pl.pallas_call(
        pack_kernel,
        in_specs=[
            pl.BlockSpec(memory_space=pltpu.SMEM),
            pl.BlockSpec((rows, features), lambda: (0, 0)),
            pl.BlockSpec((1, features), lambda: (0, 0)),
        ],
        out_specs=pl.BlockSpec((rows, features + PAD_COLS), lambda: (0, 0)),
        out_shape=jax.ShapeDtypeStruct((rows, features + PAD_COLS), jnp.bfloat16),
    )(targets, hidden, gain.reshape(1, features))


def gather_rows(packed, tensor_pos, tensor_count):
    high = tensor_count // LOW_GROUP
    if tensor_count % LOW_GROUP or high & (high - 1) or high == 1:
        return lax.all_gather(packed, "tensor", axis=0, tiled=True), lambda stats: stats
    received = [packed] + [
        lax.ppermute(packed, "tensor", [(i, i ^ (k * LOW_GROUP)) for i in range(tensor_count)])
        for k in range(1, high)
    ]
    own_high = tensor_pos // LOW_GROUP
    blocks = []
    for h in range(high):
        block = received[0]
        for k in range(1, high):
            block = jnp.where((own_high ^ h) == k, received[k], block)
        blocks.append(block)
    groups = [[h * LOW_GROUP + low for low in range(LOW_GROUP)] for h in range(high)]
    gathered = lax.all_gather(
        jnp.concatenate(blocks, axis=0), "tensor", axis=0, tiled=True, axis_index_groups=groups
    )
    own_rows = packed.shape[0]

    def restore(stats):
        stats = stats.reshape(stats.shape[0], LOW_GROUP, high, own_rows)
        return stats.transpose(0, 2, 1, 3).reshape(stats.shape[0], tensor_count * own_rows)

    return gathered, restore


def chunk_stats(normed_rows, target_rows, weight, offset):
    logits = jnp.dot(normed_rows, weight, preferred_element_type=jnp.float32)
    row_top = jnp.max(logits, axis=1)
    shifted = logits - row_top[:, None]
    weights_exp = jnp.exp(shifted)
    row_total = jnp.sum(weights_exp, axis=1)
    spread = jnp.sum(weights_exp * shifted, axis=1)
    columns = lax.iota(jnp.int32, weight.shape[1]) + offset
    is_target = target_rows[:, None] == columns[None, :]
    picked = jnp.sum(jnp.where(is_target, logits, jnp.float32(0.0)), axis=1)
    return (row_top, row_total, spread, picked)


def local_stats(normed_rows, target_rows, weight, offset):
    width = weight.shape[1]
    edges = [0] + [int(width * share) // 128 * 128 for share in CHUNK_EDGES] + [width]
    if any(b <= a for a, b in zip(edges, edges[1:])):
        edges = [0, width]
    parts = []
    for begin, end in zip(edges, edges[1:]):
        part = chunk_stats(normed_rows, target_rows, weight[:, begin:end], offset + begin)
        part, normed_rows = lax.optimization_barrier((part, normed_rows))
        parts.append(part)
    top = parts[0][0]
    for part in parts[1:]:
        top = jnp.maximum(top, part[0])
    total = jnp.zeros_like(top)
    spread = jnp.zeros_like(top)
    picked = jnp.zeros_like(top)
    for part in parts:
        factor = jnp.exp(part[0] - top)
        total = total + part[1] * factor
        spread = spread + factor * (part[2] + part[1] * (part[0] - top))
        picked = picked + part[3]
    return jnp.stack([top, total, spread, picked])


def body(hidden, gain, head_weight, targets, short_lengths, owner):
    own_rows, features = hidden.shape
    dp_pos = lax.axis_index("dp")
    dp_count = lax.axis_size("dp")
    tensor_pos = lax.axis_index("tensor")
    tensor_count = lax.axis_size("tensor")
    offset = tensor_pos * head_weight.shape[1]
    packed = pack_rows(hidden, gain, targets)
    gathered, restore = gather_rows(packed, tensor_pos, tensor_count)
    rows_normed = gathered[:, :features]
    got = gathered[:, features:features + 3].astype(jnp.int32)
    rows_targets = got[:, 0] + DIGIT * got[:, 1] + (DIGIT * DIGIT) * got[:, 2]

    stats = restore(local_stats(rows_normed, rows_targets, head_weight, offset))
    group_rows = stats.shape[1]
    devices = dp_count * tensor_count
    sent = jnp.broadcast_to(stats[None], (devices,) + stats.shape)
    everything = lax.all_to_all(sent, ("dp", "tensor"), 0, 0, tiled=True)
    everything = everything.reshape(dp_count, tensor_count, 4, group_rows)
    tops = everything[:, :, 0]
    joint = jnp.max(tops, axis=1)
    factor = jnp.exp(tops - joint[:, None, :])
    totals = everything[:, :, 1]
    row_total = jnp.sum(totals * factor, axis=1)
    spread = jnp.sum(factor * (everything[:, :, 2] + totals * (tops - joint[:, None, :])), axis=1)
    picked = jnp.sum(everything[:, :, 3], axis=1)
    total_rows = dp_count * group_rows
    row_top = joint.reshape(total_rows)
    row_total = row_total.reshape(total_rows)
    spread = spread.reshape(total_rows)
    picked = picked.reshape(total_rows)

    log_total = jnp.log(row_total)
    logprob = picked - row_top - log_total
    entropy = log_total - spread / row_total
    short_count = short_lengths.shape[0]
    long_len = total_rows - short_count * SLOT
    row_ids = lax.iota(jnp.int32, total_rows)
    past_long = row_ids - long_len
    sequence = jnp.where(row_ids < long_len, 0, 1 + past_long // SLOT)
    slot_pos = past_long % SLOT
    seq_lengths = jnp.concatenate([jnp.full((1,), long_len, jnp.int32), short_lengths])
    member = sequence[:, None] == lax.iota(jnp.int32, short_count + 1)[None, :]
    row_length = jnp.sum(jnp.where(member, seq_lengths[None, :], 0), axis=1)
    is_live = (row_ids < long_len) | (slot_pos < row_length)
    logprob = jnp.where(is_live, logprob, jnp.float32(0.0))
    entropy = jnp.where(is_live, entropy, jnp.float32(0.0))
    seq_sums = jnp.stack(
        [
            jnp.sum(jnp.where(member, logprob[:, None], jnp.float32(0.0)), axis=0),
            jnp.sum(jnp.where(member, entropy[:, None], jnp.float32(0.0)), axis=0),
        ]
    )
    seq_means = seq_sums / seq_lengths.astype(jnp.float32)[None, :]
    is_owner = owner == dp_pos
    seq_scores = jnp.where(is_owner[None, :], seq_means, jnp.float32(0.0))[None, :, :]
    me = dp_pos * tensor_count + tensor_pos
    mine = (lax.iota(jnp.int32, devices) == me)[:, None]
    own_logprob = jnp.sum(jnp.where(mine, logprob.reshape(devices, own_rows), 0.0), axis=0)
    own_entropy = jnp.sum(jnp.where(mine, entropy.reshape(devices, own_rows), 0.0), axis=0)
    return (own_logprob, own_entropy, seq_scores)


def solution(mesh):
    return jax.shard_map(
        body,
        mesh=mesh,
        in_specs=(P(("dp", "tensor"), None), P(), P(None, "tensor"), P(("dp", "tensor")), P(), P()),
        out_specs=(P(("dp", "tensor")), P(("dp", "tensor")), P("dp", None, None)),
        check_vma=False,
    )
```

```python
import jax
import jax.numpy as jnp
from jax import lax
from jax.experimental import pallas as pl
from jax.experimental.pallas import tpu as pltpu
from jax.sharding import PartitionSpec as P

SLOT = 64
DIGIT = 256
PAD_COLS = 128
LOW_GROUP = 4
CHUNK_EDGES = (0.125, 0.375, 0.625)


def pack_kernel(tgt_ref, hidden_ref, gain_ref, o_ref):
    rows, features = hidden_ref.shape
    values = hidden_ref[...].astype(jnp.float32)
    scale = lax.rsqrt(jnp.sum(values * values, axis=1, keepdims=True) / features + 1e-06)
    o_ref[:, :features] = (values * scale * gain_ref[...]).astype(jnp.bfloat16)
    place = lax.broadcasted_iota(jnp.int32, (rows, PAD_COLS), 1)
    row = lax.broadcasted_iota(jnp.int32, (rows, PAD_COLS), 0)
    target = jnp.zeros((rows, PAD_COLS), jnp.int32)
    for r in range(rows):
        target = jnp.where(row == r, tgt_ref[r], target)
    digit = jnp.where(place == 1, target // DIGIT, jnp.where(place == 2, target // (DIGIT * DIGIT), target))
    digit = jnp.where(place < 3, digit % DIGIT, 0)
    o_ref[:, features:] = digit.astype(jnp.float32).astype(jnp.bfloat16)


def pack_rows(hidden, gain, targets):
    rows, features = hidden.shape
    return pl.pallas_call(
        pack_kernel,
        in_specs=[
            pl.BlockSpec(memory_space=pltpu.SMEM),
            pl.BlockSpec((rows, features), lambda: (0, 0)),
            pl.BlockSpec((1, features), lambda: (0, 0)),
        ],
        out_specs=pl.BlockSpec((rows, features + PAD_COLS), lambda: (0, 0)),
        out_shape=jax.ShapeDtypeStruct((rows, features + PAD_COLS), jnp.bfloat16),
    )(targets, hidden, gain.reshape(1, features))


def gather_rows(packed, tensor_pos, tensor_count):
    high = tensor_count // LOW_GROUP
    if tensor_count % LOW_GROUP or high & (high - 1) or high == 1:
        return lax.all_gather(packed, "tensor", axis=0, tiled=True), lambda stats: stats
    sent = {
        k: lax.ppermute(packed, "tensor", [(i, i ^ (k * LOW_GROUP)) for i in range(tensor_count)])
        for k in range(high - 1, 0, -1)
    }
    received = [packed] + [sent[k] for k in range(1, high)]
    own_high = tensor_pos // LOW_GROUP
    blocks = []
    for h in range(high):
        block = received[0]
        for k in range(1, high):
            block = jnp.where((own_high ^ h) == k, received[k], block)
        blocks.append(block)
    groups = [[h * LOW_GROUP + low for low in range(LOW_GROUP)] for h in range(high)]
    gathered = lax.all_gather(
        jnp.concatenate(blocks, axis=0), "tensor", axis=0, tiled=True, axis_index_groups=groups
    )
    own_rows = packed.shape[0]

    def restore(stats):
        stats = stats.reshape(stats.shape[0], LOW_GROUP, high, own_rows)
        return stats.transpose(0, 2, 1, 3).reshape(stats.shape[0], tensor_count * own_rows)

    return gathered, restore


def chunk_stats(normed_rows, target_rows, weight, offset):
    logits = jnp.dot(normed_rows, weight, preferred_element_type=jnp.float32)
    row_top = jnp.max(logits, axis=1)
    shifted = logits - row_top[:, None]
    weights_exp = jnp.exp(shifted)
    row_total = jnp.sum(weights_exp, axis=1)
    spread = jnp.sum(weights_exp * shifted, axis=1)
    columns = lax.iota(jnp.int32, weight.shape[1]) + offset
    is_target = target_rows[:, None] == columns[None, :]
    picked = jnp.sum(jnp.where(is_target, logits, jnp.float32(0.0)), axis=1)
    return (row_top, row_total, spread, picked)


def local_stats(normed_rows, target_rows, weight, offset):
    width = weight.shape[1]
    edges = [0] + [int(width * share) // 128 * 128 for share in CHUNK_EDGES] + [width]
    if any(b <= a for a, b in zip(edges, edges[1:])):
        edges = [0, width]
    parts = []
    for begin, end in zip(edges, edges[1:]):
        part = chunk_stats(normed_rows, target_rows, weight[:, begin:end], offset + begin)
        part, normed_rows = lax.optimization_barrier((part, normed_rows))
        parts.append(part)
    top = parts[0][0]
    for part in parts[1:]:
        top = jnp.maximum(top, part[0])
    total = jnp.zeros_like(top)
    spread = jnp.zeros_like(top)
    picked = jnp.zeros_like(top)
    for part in parts:
        factor = jnp.exp(part[0] - top)
        total = total + part[1] * factor
        spread = spread + factor * (part[2] + part[1] * (part[0] - top))
        picked = picked + part[3]
    return jnp.stack([top, total, spread, picked])


def body(hidden, gain, head_weight, targets, short_lengths, owner):
    own_rows, features = hidden.shape
    dp_pos = lax.axis_index("dp")
    dp_count = lax.axis_size("dp")
    tensor_pos = lax.axis_index("tensor")
    tensor_count = lax.axis_size("tensor")
    offset = tensor_pos * head_weight.shape[1]
    packed = pack_rows(hidden, gain, targets)
    gathered, restore = gather_rows(packed, tensor_pos, tensor_count)
    rows_normed = gathered[:, :features]
    got = gathered[:, features:features + 3].astype(jnp.int32)
    rows_targets = got[:, 0] + DIGIT * got[:, 1] + (DIGIT * DIGIT) * got[:, 2]

    stats = restore(local_stats(rows_normed, rows_targets, head_weight, offset))
    group_rows = stats.shape[1]
    devices = dp_count * tensor_count
    sent = jnp.broadcast_to(stats[None], (devices,) + stats.shape)
    everything = lax.all_to_all(sent, ("dp", "tensor"), 0, 0, tiled=True)
    everything = everything.reshape(dp_count, tensor_count, 4, group_rows)
    tops = everything[:, :, 0]
    joint = jnp.max(tops, axis=1)
    factor = jnp.exp(tops - joint[:, None, :])
    totals = everything[:, :, 1]
    row_total = jnp.sum(totals * factor, axis=1)
    spread = jnp.sum(factor * (everything[:, :, 2] + totals * (tops - joint[:, None, :])), axis=1)
    picked = jnp.sum(everything[:, :, 3], axis=1)
    total_rows = dp_count * group_rows
    row_top = joint.reshape(total_rows)
    row_total = row_total.reshape(total_rows)
    spread = spread.reshape(total_rows)
    picked = picked.reshape(total_rows)

    log_total = jnp.log(row_total)
    logprob = picked - row_top - log_total
    entropy = log_total - spread / row_total
    short_count = short_lengths.shape[0]
    long_len = total_rows - short_count * SLOT
    row_ids = lax.iota(jnp.int32, total_rows)
    past_long = row_ids - long_len
    sequence = jnp.where(row_ids < long_len, 0, 1 + past_long // SLOT)
    slot_pos = past_long % SLOT
    seq_lengths = jnp.concatenate([jnp.full((1,), long_len, jnp.int32), short_lengths])
    member = sequence[:, None] == lax.iota(jnp.int32, short_count + 1)[None, :]
    row_length = jnp.sum(jnp.where(member, seq_lengths[None, :], 0), axis=1)
    is_live = (row_ids < long_len) | (slot_pos < row_length)
    logprob = jnp.where(is_live, logprob, jnp.float32(0.0))
    entropy = jnp.where(is_live, entropy, jnp.float32(0.0))
    seq_sums = jnp.stack(
        [
            jnp.sum(jnp.where(member, logprob[:, None], jnp.float32(0.0)), axis=0),
            jnp.sum(jnp.where(member, entropy[:, None], jnp.float32(0.0)), axis=0),
        ]
    )
    seq_means = seq_sums / seq_lengths.astype(jnp.float32)[None, :]
    is_owner = owner == dp_pos
    seq_scores = jnp.where(is_owner[None, :], seq_means, jnp.float32(0.0))[None, :, :]
    me = dp_pos * tensor_count + tensor_pos
    mine = (lax.iota(jnp.int32, devices) == me)[:, None]
    own_logprob = jnp.sum(jnp.where(mine, logprob.reshape(devices, own_rows), 0.0), axis=0)
    own_entropy = jnp.sum(jnp.where(mine, entropy.reshape(devices, own_rows), 0.0), axis=0)
    return (own_logprob, own_entropy, seq_scores)


def solution(mesh):
    return jax.shard_map(
        body,
        mesh=mesh,
        in_specs=(P(("dp", "tensor"), None), P(), P(None, "tensor"), P(("dp", "tensor")), P(), P()),
        out_specs=(P(("dp", "tensor")), P(("dp", "tensor")), P("dp", None, None)),
        check_vma=False,
    )
```
